32 devices in a mesh: ep: 16 (over z, x, core), dp: 2 (over y).
Axes of the slice: x: 2, y: 2, z: 4, core: 2. Of those that a mesh axis runs over, the one named last changes fastest.
Arguments:
- tokens: bfloat16 [1024, 4096], P('ep', 'dp'), may hold values from -6 to 6
- expert_ids: int32 [1024, 8], P('ep'), may hold values from 0 to 15, all different within a row
- gate_logits: float32 [1024, 8], P('ep'), may hold values from -6 to 6
- placement: int32 [8], replicated, may hold values from 0 to 15, as said below
- split_rows: int32 [8], replicated, may hold values from 0 to 32
- gate_up_weight: bfloat16 [16, 4096, 2, 1024], P('ep', None, None, 'dp'), may hold values from -0.09375 to 0.09375
- down_weight: bfloat16 [16, 1024, 4096], P('ep', None, 'dp'), may hold values from -0.1875 to 0.1875
- spare_gate_up: bfloat16 [16, 4096, 2, 512], P('ep', None, None, 'dp'), may hold values from -0.09375 to 0.09375
- spare_down: bfloat16 [16, 512, 4096], P('ep', None, 'dp'), may hold values from -0.1875 to 0.1875
Outputs:
- mixed: bfloat16 [1024, 4096], P('ep', 'dp')
The draws below stay inside these ranges and needn't reach their ends.
Inputs may be any that keep to these rules, and one draw needn't show every extreme that they name: `expert_ids`: each token names 8 different experts. `placement`: 8 different experts.
All inputs are finite; a program needn't handle non-finite values.
Results may differ from the reference program's by a relative error of at most 0.0058.
Values may be sent and summed in bfloat16 or wider, within the bound.
No kernel may reach another device: no remote copies, remote signals or barrier semaphores. Data moves between devices by JAX's collectives and lax.ppermute only.
A program may use at most 64 MiB of HBM per device.

```python
import jax
import jax.numpy as jnp
from jax import lax

D = 4096
FF = 1024
TOPK = 8
TOK_GRP = 64
EXPERTS = 16
REDUNDANT = 8
TOKENS = 1024
CAP = 32


def draw_placement(key, part):
    return jax.random.permutation(key, EXPERTS)[:REDUNDANT].astype(jnp.int32)


def draw_split_rows(key, part):
    first_key = jax.random.fold_in(key, 11)
    second_key = jax.random.fold_in(key, 23)
    values = jax.random.randint(first_key, (REDUNDANT,), 0, CAP + 1)
    spot = jax.random.randint(second_key, (), 0, REDUNDANT)
    order = jnp.arange(REDUNDANT)
    values = jnp.where(order == spot, CAP, values)
    values = jnp.where(order == (spot + 1) % REDUNDANT, 0, values)
    return values.astype(jnp.int32)


def shard_levels(own_key, extent, shards, low, largest):
    def one(dim, blocks):
        steps = jax.random.uniform(jax.random.fold_in(jax.random.fold_in(own_key, 6), dim), (blocks,), jnp.float32, low / len(shards), largest / len(shards))
        return jnp.repeat(jnp.exp(steps), extent[dim] // blocks).reshape((-1,) + (1,) * (len(extent) - dim - 1))

    loudness = one(*shards[0])
    for cut in shards[1:]:
        loudness = loudness * one(*cut)
    return loudness


def different_ones(stream_key, rows, amount, top, lift):
    ranking = jax.random.permutation(jax.random.fold_in(stream_key, 1), amount)
    boost = ranking
    for power in range(3):
        boost = boost * boost // amount
    boost = boost * lift // amount
    chance = jax.random.randint(jax.random.fold_in(stream_key, 2), (rows, amount), 0, 4096) + boost
    sure = jax.random.permutation(jax.random.fold_in(stream_key, 3), rows)[jnp.arange(amount) % rows]
    chance = jnp.where(jnp.arange(rows)[:, None] == sure[None, :], 1 << 14, chance)
    merit = chance * amount + jnp.arange(amount)
    return lax.top_k(merit.astype(jnp.int32), top)[1].astype(jnp.int32)


def scatter_about(key, extent, spread, bound, pieces=(), kind=jnp.bfloat16):
    result = spread * jax.random.normal(key, extent, jnp.float32)
    if pieces:
        result = result * shard_levels(key, extent, pieces, -0.22, 0.18)
    return jnp.clip(result, -bound, bound).astype(kind)


def setup_inputs(seed: int = 0) -> dict:
    splits = jax.random.split(jax.random.key(seed), 10)
    return {
        "tokens": scatter_about(splits[0], (TOKENS, D), 1.0, 6.0, ((0, 16), (1, 2))),
        "expert_ids": different_ones(splits[1], TOKENS, EXPERTS, TOPK, 4096),
        "gate_logits": scatter_about(splits[2], (TOKENS, TOPK), 1.5, 6.0, ((0, 16),), jnp.float32),
        "placement": draw_placement(jax.random.fold_in(splits[9], 71), 0),
        "split_rows": draw_split_rows(jax.random.fold_in(splits[9], 71), 0),
        "gate_up_weight": scatter_about(splits[5], (EXPERTS, D, 2, FF), D ** -0.5, 0.09375, ((0, 16), (3, 2))),
        "down_weight": scatter_about(splits[6], (EXPERTS, FF, D), FF ** -0.5, 0.1875, ((0, 16), (2, 2))),
        "spare_gate_up": scatter_about(splits[7], (2 * REDUNDANT, D, 2, FF // 2), D ** -0.5, 0.09375, ((0, 16), (3, 2))),
        "spare_down": scatter_about(splits[8], (2 * REDUNDANT, FF // 2, D), FF ** -0.5, 0.1875, ((0, 16), (2, 2))),
    }


def assign_slots(expert_ids, placement, split_rows):
    per_group = TOK_GRP * TOPK
    chosen_ids = expert_ids.reshape(-1, per_group)
    ordinal = jnp.arange(per_group, dtype=jnp.int32)
    earlier = ordinal[None, :] < ordinal[:, None]
    same_expert = chosen_ids[:, :, None] == chosen_ids[:, None, :]
    pair_rank = jnp.sum(jnp.where(same_expert & earlier[None], 1, 0), axis=2).astype(jnp.int32)
    is_match = chosen_ids[:, :, None] == placement[None, None, :]
    is_hot = jnp.any(is_match, axis=2)
    copy_index = jnp.sum(jnp.where(is_match, jnp.arange(REDUNDANT, dtype=jnp.int32)[None, None, :], 0), axis=2).astype(jnp.int32)
    split_here = jnp.sum(jnp.where(is_match, split_rows[None, None, :], 0), axis=2).astype(jnp.int32)
    to_copy = is_hot & (pair_rank >= split_here)
    slot_of = jnp.where(to_copy, EXPERTS + copy_index, chosen_ids).astype(jnp.int32)
    position = jnp.where(to_copy, pair_rank - split_here, pair_rank).astype(jnp.int32)
    kept_mask = position < CAP
    return slot_of, position, kept_mask


def run_slot(token_rows, both_weight, down_part):
    gate_both = jnp.dot(token_rows, both_weight.reshape(D, 2 * FF), preferred_element_type=jnp.float32)
    gate_both = gate_both.reshape(token_rows.shape[0], 2, FF)
    hidden = (jax.nn.silu(gate_both[:, 0, :]) * gate_both[:, 1, :]).astype(jnp.bfloat16)
    return jnp.dot(hidden, down_part, preferred_element_type=jnp.float32).astype(jnp.bfloat16)


def reference(tokens, expert_ids, gate_logits, placement, split_rows, gate_up_weight, down_weight, spare_gate_up, spare_down):
    gate_score = jax.nn.sigmoid(gate_logits.astype(jnp.float32))
    gate_weight = 2.5 * gate_score / jnp.sum(gate_score, axis=1, keepdims=True)
    slot_of, position, kept_mask = assign_slots(expert_ids, placement, split_rows)
    groups = TOKENS // TOK_GRP
    per_group = TOK_GRP * TOPK
    slot_count = EXPERTS + REDUNDANT
    slot_total = slot_count * groups * CAP
    group_of = jnp.arange(groups, dtype=jnp.int32)[:, None]
    flat_index = ((slot_of * groups + group_of) * CAP + position).astype(jnp.int32)
    owner_token = (group_of * TOK_GRP + jnp.arange(per_group, dtype=jnp.int32)[None, :] // TOPK).astype(jnp.int32)
    row_table = jnp.full((slot_total,), TOKENS, jnp.int32)
    row_table = row_table.at[jnp.where(kept_mask, flat_index, slot_total)].set(owner_token, mode="drop")
    row_table = row_table.reshape(slot_count, groups * CAP)
    padded = jnp.concatenate([tokens, jnp.zeros((1, D), tokens.dtype)], axis=0)
    spare_gu_all = spare_gate_up.reshape(REDUNDANT, 2, D, 2, FF // 2)
    spare_dn_all = spare_down.reshape(REDUNDANT, 2, FF // 2, D)

    def home_slot(slot_index):
        token_rows = jnp.take(padded, row_table[slot_index], axis=0)
        return run_slot(token_rows, gate_up_weight[slot_index], down_weight[slot_index])

    def spare_slot(spare_index):
        token_rows = jnp.take(padded, row_table[EXPERTS + spare_index], axis=0)
        both_weight = jnp.transpose(spare_gu_all[spare_index], (1, 2, 0, 3)).reshape(D, 2, FF)
        down_part = spare_dn_all[spare_index].reshape(FF, D)
        return run_slot(token_rows, both_weight, down_part)

    home_out = lax.map(home_slot, jnp.arange(EXPERTS, dtype=jnp.int32))
    spare_out = lax.map(spare_slot, jnp.arange(REDUNDANT, dtype=jnp.int32))
    flat_out = jnp.concatenate([home_out, spare_out], axis=0).reshape(slot_total, D)
    picked = jnp.take(flat_out, jnp.where(kept_mask, flat_index, 0), axis=0)
    kept_weight = jnp.where(kept_mask, gate_weight.reshape(groups, per_group), 0.0)
    mixed = jnp.sum((kept_weight[:, :, None] * picked.astype(jnp.float32)).reshape(TOKENS, TOPK, D), axis=1)
    return mixed.astype(jnp.bfloat16)
```

```python
import jax
import jax.numpy as jnp
from jax import lax
from jax.sharding import PartitionSpec as P


def gate_up(row_block, weight):
    gate_both = jnp.einsum("rd,djf->rjf", row_block, weight, preferred_element_type=jnp.float32)
    return (jax.nn.silu(gate_both[:, 0, :]) * gate_both[:, 1, :]).astype(jnp.bfloat16)


def slot_tables(ids, target, low, limit, capacity, top_count):
    groups, per_group = ids.shape
    hit = ids == target
    ordinal = jnp.arange(per_group, dtype=jnp.int32)
    earlier = (ordinal[None, :] < ordinal[:, None]).astype(jnp.bfloat16)
    rank = jnp.einsum(
        "pq,gq->gp", earlier, hit.astype(jnp.bfloat16), preferred_element_type=jnp.float32
    ).astype(jnp.int32)
    position = rank - low
    kept = hit & (position >= 0) & (position < limit)
    group_tokens = per_group // top_count
    token = jnp.arange(groups, dtype=jnp.int32)[:, None] * group_tokens + ordinal[None, :] // top_count
    slots = jnp.arange(capacity, dtype=jnp.int32)
    sel = kept[:, :, None] & (position[:, :, None] == slots[None, None, :])
    row_of_slot = jnp.sum(jnp.where(sel, token[:, :, None], 0), axis=1)
    flat = jnp.arange(groups, dtype=jnp.int32)[:, None] * capacity + position
    return row_of_slot.reshape(-1), kept, flat


def per_token(kept, flat, weight, group_tokens, top_count):
    groups = kept.shape[0]
    kept = kept.reshape(groups * group_tokens, top_count)
    flat = flat.reshape(groups * group_tokens, top_count)
    index = jnp.sum(jnp.where(kept, flat, 0), axis=1)
    scale = jnp.sum(jnp.where(kept, weight, 0.0), axis=1)
    return index, scale


def per_device(
    tokens,
    expert_ids,
    gate_logits,
    placement,
    split_rows,
    gate_up_weight,
    down_weight,
    spare_gate_up,
    spare_down,
):
    ep_count = lax.axis_size("ep")
    me = lax.axis_index("ep")
    group_tokens = tokens.shape[0]
    top_count = expert_ids.shape[1]
    spares = placement.shape[0]
    halves = spare_gate_up.shape[0] * ep_count // spares
    capacity = group_tokens * top_count // ep_count
    per_group = group_tokens * top_count

    whole_rows = lax.all_gather(tokens, "dp", axis=1, tiled=True)
    every_row = lax.all_gather(whole_rows, "ep", axis=0, tiled=True)
    every_id = lax.all_gather(expert_ids, "ep", axis=0, tiled=True)
    every_logit = lax.all_gather(gate_logits, "ep", axis=0, tiled=True)
    ids = every_id.reshape(ep_count, per_group)

    gate_score = jax.nn.sigmoid(every_logit)
    gate_weight = 2.5 * gate_score / jnp.sum(gate_score, axis=1, keepdims=True)

    is_match = placement == me
    home_limit = jnp.where(
        jnp.any(is_match), jnp.minimum(jnp.sum(jnp.where(is_match, split_rows, 0)), capacity), capacity
    )
    home_rows_of, home_kept, home_flat = slot_tables(
        ids, me, 0, home_limit, capacity, top_count
    )
    spare_index = me // halves
    spare_rows_of, spare_kept, spare_flat = slot_tables(
        ids, placement[spare_index], split_rows[spare_index], capacity, capacity, top_count
    )

    home_rows = jnp.take(every_row, home_rows_of, axis=0)
    spare_rows = jnp.take(every_row, spare_rows_of, axis=0)
    home_hidden = gate_up(home_rows, gate_up_weight[0])
    spare_hidden = gate_up(spare_rows, spare_gate_up[0])
    home_hidden = lax.all_gather(home_hidden, "dp", axis=1, tiled=True)
    spare_hidden = lax.all_gather(spare_hidden, "dp", axis=1, tiled=True)
    home_out = jnp.dot(home_hidden, down_weight[0], preferred_element_type=jnp.float32)
    home_out = home_out.astype(jnp.bfloat16).astype(jnp.float32)
    spare_out = jnp.dot(spare_hidden, spare_down[0], preferred_element_type=jnp.float32)

    home_at, home_scale = per_token(home_kept, home_flat, gate_weight, group_tokens, top_count)
    spare_at, spare_scale = per_token(spare_kept, spare_flat, gate_weight, group_tokens, top_count)
    partial = home_scale[:, None] * jnp.take(home_out, home_at, axis=0) + spare_scale[
        :, None
    ] * jnp.take(spare_out, spare_at, axis=0)
    mixed = lax.psum_scatter(partial, "ep", scatter_dimension=0, tiled=True)
    return mixed.astype(jnp.bfloat16)


def solution(mesh):
    return jax.shard_map(
        per_device,
        mesh=mesh,
        in_specs=(
            P("ep", "dp"),
            P("ep", None),
            P("ep", None),
            P(),
            P(),
            P("ep", None, None, "dp"),
            P("ep", None, "dp"),
            P("ep", None, None, "dp"),
            P("ep", None, "dp"),
        ),
        out_specs=P("ep", "dp"),
        check_vma=False,
    )
```

```python
import jax
import jax.numpy as jnp
from jax import lax
from jax.sharding import PartitionSpec as P


def gate_up(row_block, weight):
    gate_both = jnp.einsum("rd,djf->rjf", row_block, weight, preferred_element_type=jnp.float32)
    return (jax.nn.silu(gate_both[:, 0, :]) * gate_both[:, 1, :]).astype(jnp.bfloat16)


def slot_tables(ids, target, low, limit, capacity, top_count):
    groups, per_group = ids.shape
    hit = ids == target
    ordinal = jnp.arange(per_group, dtype=jnp.int32)
    earlier = (ordinal[None, :] < ordinal[:, None]).astype(jnp.bfloat16)
    rank = jnp.einsum(
        "pq,gq->gp", earlier, hit.astype(jnp.bfloat16), preferred_element_type=jnp.float32
    ).astype(jnp.int32)
    position = rank - low
    kept = hit & (position >= 0) & (position < limit)
    group_tokens = per_group // top_count
    token = jnp.arange(groups, dtype=jnp.int32)[:, None] * group_tokens + ordinal[None, :] // top_count
    slots = jnp.arange(capacity, dtype=jnp.int32)
    sel = kept[:, :, None] & (position[:, :, None] == slots[None, None, :])
    row_of_slot = jnp.sum(jnp.where(sel, token[:, :, None], 0), axis=1)
    flat = jnp.arange(groups, dtype=jnp.int32)[:, None] * capacity + position
    return row_of_slot.reshape(-1), kept, flat


def per_token(kept, flat, weight, group_tokens, top_count):
    groups = kept.shape[0]
    kept = kept.reshape(groups * group_tokens, top_count)
    flat = flat.reshape(groups * group_tokens, top_count)
    index = jnp.sum(jnp.where(kept, flat, 0), axis=1)
    scale = jnp.sum(jnp.where(kept, weight, 0.0), axis=1)
    return index, scale


def one_hot(index, size):
    return (index[:, None] == jnp.arange(size, dtype=jnp.int32)[None, :]).astype(jnp.bfloat16)


def side_columns(expert_ids, gate_logits):
    high = gate_logits.astype(jnp.bfloat16)
    rest = gate_logits - high.astype(jnp.float32)
    middle = rest.astype(jnp.bfloat16)
    low = (rest - middle.astype(jnp.float32)).astype(jnp.bfloat16)
    columns = jnp.concatenate([expert_ids.astype(jnp.bfloat16), high, middle, low], axis=1)
    width = -columns.shape[1] % 128
    return jnp.pad(columns, ((0, 0), (0, width)))


def per_device(
    tokens,
    expert_ids,
    gate_logits,
    placement,
    split_rows,
    gate_up_weight,
    down_weight,
    spare_gate_up,
    spare_down,
):
    ep_count = lax.axis_size("ep")
    me = lax.axis_index("ep")
    group_tokens = tokens.shape[0]
    top_count = expert_ids.shape[1]
    spares = placement.shape[0]
    halves = spare_gate_up.shape[0] * ep_count // spares
    capacity = group_tokens * top_count // ep_count
    per_group = group_tokens * top_count

    d_model = tokens.shape[1] * lax.axis_size("dp")
    whole_rows = lax.all_gather(tokens, "dp", axis=1, tiled=True)
    packed = jnp.concatenate([whole_rows, side_columns(expert_ids, gate_logits)], axis=1)
    every_row = lax.all_gather(packed, "ep", axis=0, tiled=True)
    all_tokens = every_row.shape[0]
    ids = every_row[:, d_model : d_model + top_count].astype(jnp.int32)
    parts = every_row[:, d_model + top_count : d_model + 4 * top_count].astype(jnp.float32)
    every_logit = (
        parts[:, :top_count] + parts[:, top_count : 2 * top_count]
    ) + parts[:, 2 * top_count :]
    ids = ids.reshape(ep_count, per_group)

    gate_score = jax.nn.sigmoid(every_logit)
    gate_weight = 2.5 * gate_score / jnp.sum(gate_score, axis=1, keepdims=True)

    is_match = placement == me
    home_limit = jnp.where(
        jnp.any(is_match), jnp.minimum(jnp.sum(jnp.where(is_match, split_rows, 0)), capacity), capacity
    )
    home_rows_of, home_kept, home_flat = slot_tables(
        ids, me, 0, home_limit, capacity, top_count
    )
    spare_index = me // halves
    spare_rows_of, spare_kept, spare_flat = slot_tables(
        ids, placement[spare_index], split_rows[spare_index], capacity, capacity, top_count
    )

    slot_rows = home_rows_of.shape[0]
    pick = one_hot(jnp.concatenate([home_rows_of, spare_rows_of]), all_tokens)
    rows = jnp.dot(pick, every_row, preferred_element_type=jnp.float32).astype(jnp.bfloat16)
    home_hidden = gate_up(rows[:slot_rows, :d_model], gate_up_weight[0])
    spare_hidden = gate_up(rows[slot_rows:, :d_model], spare_gate_up[0])
    home_hidden = lax.all_gather(home_hidden, "dp", axis=1, tiled=True)
    spare_hidden = lax.all_gather(spare_hidden, "dp", axis=1, tiled=True)
    home_out = jnp.dot(home_hidden, down_weight[0], preferred_element_type=jnp.float32)
    home_out = home_out.astype(jnp.bfloat16)
    spare_out = jnp.dot(spare_hidden, spare_down[0], preferred_element_type=jnp.float32)
    spare_high = spare_out.astype(jnp.bfloat16)
    spare_low = (spare_out - spare_high.astype(jnp.float32)).astype(jnp.bfloat16)

    home_at, home_scale = per_token(home_kept, home_flat, gate_weight, group_tokens, top_count)
    spare_at, spare_scale = per_token(spare_kept, spare_flat, gate_weight, group_tokens, top_count)
    home_pick = one_hot(home_at, slot_rows)
    spare_pick = one_hot(spare_at, slot_rows)
    home_term = jnp.dot(home_pick, home_out, preferred_element_type=jnp.float32)
    spare_term = jnp.dot(
        jnp.concatenate([spare_pick, spare_pick], axis=1),
        jnp.concatenate([spare_high, spare_low], axis=0),
        preferred_element_type=jnp.float32,
    )
    partial = home_scale[:, None] * home_term + spare_scale[:, None] * spare_term
    mixed = lax.psum_scatter(partial, "ep", scatter_dimension=0, tiled=True)
    return mixed.astype(jnp.bfloat16)


def solution(mesh):
    return jax.shard_map(
        per_device,
        mesh=mesh,
        in_specs=(
            P("ep", "dp"),
            P("ep", None),
            P("ep", None),
            P(),
            P(),
            P("ep", None, None, "dp"),
            P("ep", None, "dp"),
            P("ep", None, None, "dp"),
            P("ep", None, "dp"),
        ),
        out_specs=P("ep", "dp"),
        check_vma=False,
    )
```

```python
import jax
import jax.numpy as jnp
from jax import lax
from jax.sharding import PartitionSpec as P


def gate_up(row_block, weight):
    gate_both = jnp.einsum("rd,djf->rjf", row_block, weight, preferred_element_type=jnp.float32)
    return (jax.nn.silu(gate_both[:, 0, :]) * gate_both[:, 1, :]).astype(jnp.bfloat16)


def slot_tables(ids, target, low, limit, capacity, top_count):
    groups, per_group = ids.shape
    hit = ids == target
    ordinal = jnp.arange(per_group, dtype=jnp.int32)
    earlier = (ordinal[None, :] < ordinal[:, None]).astype(jnp.bfloat16)
    rank = jnp.einsum(
        "pq,gq->gp", earlier, hit.astype(jnp.bfloat16), preferred_element_type=jnp.float32
    ).astype(jnp.int32)
    position = rank - low
    kept = hit & (position >= 0) & (position < limit)
    group_tokens = per_group // top_count
    token = jnp.arange(groups, dtype=jnp.int32)[:, None] * group_tokens + ordinal[None, :] // top_count
    slots = jnp.arange(capacity, dtype=jnp.int32)
    sel = kept[:, :, None] & (position[:, :, None] == slots[None, None, :])
    row_of_slot = jnp.sum(jnp.where(sel, token[:, :, None], 0), axis=1)
    flat = jnp.arange(groups, dtype=jnp.int32)[:, None] * capacity + position
    return row_of_slot.reshape(-1), kept, flat


def per_token(kept, flat, weight, group_tokens, top_count):
    groups = kept.shape[0]
    kept = kept.reshape(groups * group_tokens, top_count)
    flat = flat.reshape(groups * group_tokens, top_count)
    index = jnp.sum(jnp.where(kept, flat, 0), axis=1)
    scale = jnp.sum(jnp.where(kept, weight, 0.0), axis=1)
    return index, scale


def one_hot(index, size):
    return (index[:, None] == jnp.arange(size, dtype=jnp.int32)[None, :]).astype(jnp.bfloat16)


def side_columns(expert_ids, gate_logits):
    high = gate_logits.astype(jnp.bfloat16)
    rest = gate_logits - high.astype(jnp.float32)
    middle = rest.astype(jnp.bfloat16)
    low = (rest - middle.astype(jnp.float32)).astype(jnp.bfloat16)
    columns = jnp.concatenate([expert_ids.astype(jnp.bfloat16), high, middle, low], axis=1)
    width = -columns.shape[1] % 128
    return jnp.pad(columns, ((0, 0), (0, width)))


def per_device(
    tokens,
    expert_ids,
    gate_logits,
    placement,
    split_rows,
    gate_up_weight,
    down_weight,
    spare_gate_up,
    spare_down,
):
    ep_count = lax.axis_size("ep")
    me = lax.axis_index("ep")
    group_tokens = tokens.shape[0]
    top_count = expert_ids.shape[1]
    spares = placement.shape[0]
    halves = spare_gate_up.shape[0] * ep_count // spares
    capacity = group_tokens * top_count // ep_count
    per_group = group_tokens * top_count

    d_model = tokens.shape[1] * lax.axis_size("dp")
    whole_rows = lax.all_gather(tokens, "dp", axis=1, tiled=True)
    packed = jnp.concatenate([whole_rows, side_columns(expert_ids, gate_logits)], axis=1)
    every_row = lax.all_gather(packed, "ep", axis=0, tiled=True)
    all_tokens = every_row.shape[0]
    ids = every_row[:, d_model : d_model + top_count].astype(jnp.int32)
    parts = every_row[:, d_model + top_count : d_model + 4 * top_count].astype(jnp.float32)
    every_logit = (
        parts[:, :top_count] + parts[:, top_count : 2 * top_count]
    ) + parts[:, 2 * top_count :]
    ids = ids.reshape(ep_count, per_group)

    gate_score = jax.nn.sigmoid(every_logit)
    gate_weight = 2.5 * gate_score / jnp.sum(gate_score, axis=1, keepdims=True)

    is_match = placement == me
    home_limit = jnp.where(
        jnp.any(is_match), jnp.minimum(jnp.sum(jnp.where(is_match, split_rows, 0)), capacity), capacity
    )
    home_rows_of, home_kept, home_flat = slot_tables(
        ids, me, 0, home_limit, capacity, top_count
    )
    spare_index = me // halves
    spare_rows_of, spare_kept, spare_flat = slot_tables(
        ids, placement[spare_index], split_rows[spare_index], capacity, capacity, top_count
    )

    slot_rows = home_rows_of.shape[0]
    pick = one_hot(jnp.concatenate([home_rows_of, spare_rows_of]), all_tokens)
    rows = jnp.dot(pick, every_row, preferred_element_type=jnp.float32).astype(jnp.bfloat16)
    home_hidden = gate_up(rows[:slot_rows, :d_model], gate_up_weight[0])
    spare_hidden = gate_up(rows[slot_rows:, :d_model], spare_gate_up[0])
    home_hidden = lax.all_gather(home_hidden, "dp", axis=1, tiled=True)
    spare_hidden = lax.all_gather(spare_hidden, "dp", axis=1, tiled=True)
    home_out = jnp.dot(home_hidden, down_weight[0], preferred_element_type=jnp.float32)
    home_out = home_out.astype(jnp.bfloat16)
    spare_out = jnp.dot(spare_hidden, spare_down[0], preferred_element_type=jnp.float32)
    spare_high = spare_out.astype(jnp.bfloat16)
    spare_low = (spare_out - spare_high.astype(jnp.float32)).astype(jnp.bfloat16)

    home_at, home_scale = per_token(home_kept, home_flat, gate_weight, group_tokens, top_count)
    spare_at, spare_scale = per_token(spare_kept, spare_flat, gate_weight, group_tokens, top_count)
    home_pick = one_hot(home_at, slot_rows)
    spare_pick = one_hot(spare_at, slot_rows)
    home_term = jnp.dot(home_pick, home_out, preferred_element_type=jnp.float32)
    spare_term = jnp.dot(
        jnp.concatenate([spare_pick, spare_pick], axis=1),
        jnp.concatenate([spare_high, spare_low], axis=0),
        preferred_element_type=jnp.float32,
    )
    partial = home_scale[:, None] * home_term + spare_scale[:, None] * spare_term
    mixed = lax.psum_scatter(partial.astype(jnp.bfloat16), "ep", scatter_dimension=0, tiled=True)
    return mixed.astype(jnp.bfloat16)


def solution(mesh):
    return jax.shard_map(
        per_device,
        mesh=mesh,
        in_specs=(
            P("ep", "dp"),
            P("ep", None),
            P("ep", None),
            P(),
            P(),
            P("ep", None, None, "dp"),
            P("ep", None, "dp"),
            P("ep", None, None, "dp"),
            P("ep", None, "dp"),
        ),
        out_specs=P("ep", "dp"),
        check_vma=False,
    )
```

```python
import jax
import jax.numpy as jnp
from jax import lax
from jax.sharding import PartitionSpec as P


def gate_up(rows_own, rows_other, weight, dp_me, order):
    dp_count = order.shape[0] + 1
    blocks = weight.reshape(dp_count, -1, weight.shape[1], weight.shape[2])
    own = jnp.einsum(
        "rd,djf->rjf", rows_own, blocks[dp_me], preferred_element_type=jnp.float32
    )
    rest = jnp.einsum(
        "rbd,bdjf->rjf", rows_other, jnp.take(blocks, order, axis=0), preferred_element_type=jnp.float32
    )
    gate_both = own + rest
    return (jax.nn.silu(gate_both[:, 0, :]) * gate_both[:, 1, :]).astype(jnp.bfloat16)


def slot_tables(ids, target, low, limit, capacity, top_count):
    groups, per_group = ids.shape
    hit = ids == target
    ordinal = jnp.arange(per_group, dtype=jnp.int32)
    earlier = (ordinal[None, :] < ordinal[:, None]).astype(jnp.bfloat16)
    rank = jnp.einsum(
        "pq,gq->gp", earlier, hit.astype(jnp.bfloat16), preferred_element_type=jnp.float32
    ).astype(jnp.int32)
    position = rank - low
    kept = hit & (position >= 0) & (position < limit)
    group_tokens = per_group // top_count
    token = jnp.arange(groups, dtype=jnp.int32)[:, None] * group_tokens + ordinal[None, :] // top_count
    slots = jnp.arange(capacity, dtype=jnp.int32)
    sel = kept[:, :, None] & (position[:, :, None] == slots[None, None, :])
    row_of_slot = jnp.sum(jnp.where(sel, token[:, :, None], 0), axis=1)
    flat = jnp.arange(groups, dtype=jnp.int32)[:, None] * capacity + position
    return row_of_slot.reshape(-1), kept, flat


def per_token(kept, flat, weight, group_tokens, top_count):
    groups = kept.shape[0]
    kept = kept.reshape(groups * group_tokens, top_count)
    flat = flat.reshape(groups * group_tokens, top_count)
    index = jnp.sum(jnp.where(kept, flat, 0), axis=1)
    scale = jnp.sum(jnp.where(kept, weight, 0.0), axis=1)
    return index, scale


def one_hot(index, size):
    return (index[:, None] == jnp.arange(size, dtype=jnp.int32)[None, :]).astype(jnp.bfloat16)


def side_columns(expert_ids, gate_logits):
    high = gate_logits.astype(jnp.bfloat16)
    rest = gate_logits - high.astype(jnp.float32)
    middle = rest.astype(jnp.bfloat16)
    low = (rest - middle.astype(jnp.float32)).astype(jnp.bfloat16)
    columns = jnp.concatenate([expert_ids.astype(jnp.bfloat16), high, middle, low], axis=1)
    width = -columns.shape[1] % 128
    return jnp.pad(columns, ((0, 0), (0, width)))


def per_device(
    tokens,
    expert_ids,
    gate_logits,
    placement,
    split_rows,
    gate_up_weight,
    down_weight,
    spare_gate_up,
    spare_down,
):
    ep_count = lax.axis_size("ep")
    me = lax.axis_index("ep")
    group_tokens = tokens.shape[0]
    top_count = expert_ids.shape[1]
    spares = placement.shape[0]
    halves = spare_gate_up.shape[0] * ep_count // spares
    capacity = group_tokens * top_count // ep_count
    per_group = group_tokens * top_count

    dp_count = lax.axis_size("dp")
    dp_me = lax.axis_index("dp")
    block = tokens.shape[1]
    own_columns = jnp.concatenate([tokens, side_columns(expert_ids, gate_logits)], axis=1)
    first = lax.all_gather(own_columns, "ep", axis=0, tiled=True)
    blocks = lax.all_gather(tokens, "dp", axis=0)
    order = (dp_me + 1 + jnp.arange(dp_count - 1, dtype=jnp.int32)) % dp_count
    others = jnp.transpose(jnp.take(blocks, order, axis=0), (1, 0, 2)).reshape(group_tokens, -1)
    second = lax.all_gather(others, "ep", axis=0, tiled=True)
    all_tokens = first.shape[0]
    ids = first[:, block : block + top_count].astype(jnp.int32)
    parts = first[:, block + top_count : block + 4 * top_count].astype(jnp.float32)
    every_logit = (
        parts[:, :top_count] + parts[:, top_count : 2 * top_count]
    ) + parts[:, 2 * top_count :]
    ids = ids.reshape(ep_count, per_group)

    gate_score = jax.nn.sigmoid(every_logit)
    gate_weight = 2.5 * gate_score / jnp.sum(gate_score, axis=1, keepdims=True)

    is_match = placement == me
    home_limit = jnp.where(
        jnp.any(is_match), jnp.minimum(jnp.sum(jnp.where(is_match, split_rows, 0)), capacity), capacity
    )
    home_rows_of, home_kept, home_flat = slot_tables(
        ids, me, 0, home_limit, capacity, top_count
    )
    spare_index = me // halves
    spare_rows_of, spare_kept, spare_flat = slot_tables(
        ids, placement[spare_index], split_rows[spare_index], capacity, capacity, top_count
    )

    slot_rows = home_rows_of.shape[0]
    pick = one_hot(jnp.concatenate([home_rows_of, spare_rows_of]), all_tokens)
    rows_own = jnp.dot(pick, first, preferred_element_type=jnp.float32).astype(jnp.bfloat16)
    rows_other = jnp.dot(pick, second, preferred_element_type=jnp.float32).astype(jnp.bfloat16)
    rows_other = rows_other.reshape(2 * slot_rows, dp_count - 1, block)
    home_hidden = gate_up(
        rows_own[:slot_rows, :block], rows_other[:slot_rows], gate_up_weight[0], dp_me, order
    )
    spare_hidden = gate_up(
        rows_own[slot_rows:, :block], rows_other[slot_rows:], spare_gate_up[0], dp_me, order
    )
    home_units = home_hidden.shape[1]
    hidden = lax.all_gather(
        jnp.concatenate([home_hidden, spare_hidden], axis=1), "dp", axis=1, tiled=True
    ).reshape(slot_rows, dp_count, -1)
    home_out = jnp.einsum(
        "rdf,dfe->re",
        hidden[:, :, :home_units],
        down_weight[0].reshape(dp_count, home_units, -1),
        preferred_element_type=jnp.float32,
    )
    home_out = home_out.astype(jnp.bfloat16)
    spare_out = jnp.einsum(
        "rdf,dfe->re",
        hidden[:, :, home_units:],
        spare_down[0].reshape(dp_count, -1, spare_down.shape[2]),
        preferred_element_type=jnp.float32,
    )
    spare_high = spare_out.astype(jnp.bfloat16)
    spare_low = (spare_out - spare_high.astype(jnp.float32)).astype(jnp.bfloat16)

    home_at, home_scale = per_token(home_kept, home_flat, gate_weight, group_tokens, top_count)
    spare_at, spare_scale = per_token(spare_kept, spare_flat, gate_weight, group_tokens, top_count)
    home_pick = one_hot(home_at, slot_rows)
    spare_pick = one_hot(spare_at, slot_rows)
    home_term = jnp.dot(home_pick, home_out, preferred_element_type=jnp.float32)
    spare_term = jnp.dot(
        jnp.concatenate([spare_pick, spare_pick], axis=1),
        jnp.concatenate([spare_high, spare_low], axis=0),
        preferred_element_type=jnp.float32,
    )
    partial = home_scale[:, None] * home_term + spare_scale[:, None] * spare_term
    mixed = lax.psum_scatter(partial.astype(jnp.bfloat16), "ep", scatter_dimension=0, tiled=True)
    return mixed.astype(jnp.bfloat16)


def solution(mesh):
    return jax.shard_map(
        per_device,
        mesh=mesh,
        in_specs=(
            P("ep", "dp"),
            P("ep", None),
            P("ep", None),
            P(),
            P(),
            P("ep", None, None, "dp"),
            P("ep", None, "dp"),
            P("ep", None, None, "dp"),
            P("ep", None, "dp"),
        ),
        out_specs=P("ep", "dp"),
        check_vma=False,
    )
```

```python
import jax
import jax.numpy as jnp
from jax import lax
from jax.sharding import PartitionSpec as P


def gate_up(row_block, weight):
    gate_both = jnp.einsum("rd,djf->rjf", row_block, weight, preferred_element_type=jnp.float32)
    return (jax.nn.silu(gate_both[:, 0, :]) * gate_both[:, 1, :]).astype(jnp.bfloat16)


def slot_tables(ids, target, low, limit, capacity, top_count):
    groups, per_group = ids.shape
    hit = ids == target
    ordinal = jnp.arange(per_group, dtype=jnp.int32)
    earlier = (ordinal[None, :] < ordinal[:, None]).astype(jnp.bfloat16)
    rank = jnp.einsum(
        "pq,gq->gp", earlier, hit.astype(jnp.bfloat16), preferred_element_type=jnp.float32
    ).astype(jnp.int32)
    position = rank - low
    kept = hit & (position >= 0) & (position < limit)
    group_tokens = per_group // top_count
    token = jnp.arange(groups, dtype=jnp.int32)[:, None] * group_tokens + ordinal[None, :] // top_count
    slots = jnp.arange(capacity, dtype=jnp.int32)
    sel = kept[:, :, None] & (position[:, :, None] == slots[None, None, :])
    row_of_slot = jnp.sum(jnp.where(sel, token[:, :, None], 0), axis=1)
    flat = jnp.arange(groups, dtype=jnp.int32)[:, None] * capacity + position
    return row_of_slot.reshape(-1), kept, flat


def per_token(kept, flat, weight, group_tokens, top_count):
    groups = kept.shape[0]
    kept = kept.reshape(groups * group_tokens, top_count)
    flat = flat.reshape(groups * group_tokens, top_count)
    index = jnp.sum(jnp.where(kept, flat, 0), axis=1)
    scale = jnp.sum(jnp.where(kept, weight, 0.0), axis=1)
    return index, scale


def one_hot(index, size):
    return (index[:, None] == jnp.arange(size, dtype=jnp.int32)[None, :]).astype(jnp.bfloat16)


def side_columns(expert_ids, gate_logits):
    high = gate_logits.astype(jnp.bfloat16)
    rest = gate_logits - high.astype(jnp.float32)
    middle = rest.astype(jnp.bfloat16)
    low = (rest - middle.astype(jnp.float32)).astype(jnp.bfloat16)
    columns = jnp.concatenate([expert_ids.astype(jnp.bfloat16), high, middle, low], axis=1)
    width = -columns.shape[1] % 128
    return jnp.pad(columns, ((0, 0), (0, width)))


def gather_dp(block, axis):
    if lax.axis_size("dp") != 2:
        return lax.all_gather(block, "dp", axis=axis, tiled=True)
    partner = lax.ppermute(block, "dp", perm=[(0, 1), (1, 0)])
    first = lax.axis_index("dp") == 0
    low = jnp.where(first, block, partner)
    high = jnp.where(first, partner, block)
    return jnp.concatenate([low, high], axis=axis)


def per_device(
    tokens,
    expert_ids,
    gate_logits,
    placement,
    split_rows,
    gate_up_weight,
    down_weight,
    spare_gate_up,
    spare_down,
):
    ep_count = lax.axis_size("ep")
    me = lax.axis_index("ep")
    group_tokens = tokens.shape[0]
    top_count = expert_ids.shape[1]
    spares = placement.shape[0]
    halves = spare_gate_up.shape[0] * ep_count // spares
    capacity = group_tokens * top_count // ep_count
    per_group = group_tokens * top_count

    d_model = tokens.shape[1] * lax.axis_size("dp")
    whole_rows = gather_dp(tokens, 1)
    packed = jnp.concatenate([whole_rows, side_columns(expert_ids, gate_logits)], axis=1)
    every_row = lax.all_gather(packed, "ep", axis=0, tiled=True)
    all_tokens = every_row.shape[0]
    ids = every_row[:, d_model : d_model + top_count].astype(jnp.int32)
    parts = every_row[:, d_model + top_count : d_model + 4 * top_count].astype(jnp.float32)
    every_logit = (
        parts[:, :top_count] + parts[:, top_count : 2 * top_count]
    ) + parts[:, 2 * top_count :]
    ids = ids.reshape(ep_count, per_group)

    gate_score = jax.nn.sigmoid(every_logit)
    gate_weight = 2.5 * gate_score / jnp.sum(gate_score, axis=1, keepdims=True)

    is_match = placement == me
    home_limit = jnp.where(
        jnp.any(is_match), jnp.minimum(jnp.sum(jnp.where(is_match, split_rows, 0)), capacity), capacity
    )
    home_rows_of, home_kept, home_flat = slot_tables(
        ids, me, 0, home_limit, capacity, top_count
    )
    spare_index = me // halves
    spare_rows_of, spare_kept, spare_flat = slot_tables(
        ids, placement[spare_index], split_rows[spare_index], capacity, capacity, top_count
    )

    slot_rows = home_rows_of.shape[0]
    pick = one_hot(jnp.concatenate([home_rows_of, spare_rows_of]), all_tokens)
    rows = jnp.dot(pick, every_row, preferred_element_type=jnp.float32).astype(jnp.bfloat16)
    home_hidden = gate_up(rows[:slot_rows, :d_model], gate_up_weight[0])
    spare_hidden = gate_up(rows[slot_rows:, :d_model], spare_gate_up[0])
    home_hidden = lax.all_gather(home_hidden, "dp", axis=1, tiled=True)
    spare_hidden = gather_dp(spare_hidden, 1)
    home_out = jnp.dot(home_hidden, down_weight[0], preferred_element_type=jnp.float32)
    home_out = home_out.astype(jnp.bfloat16)
    spare_out = jnp.dot(spare_hidden, spare_down[0], preferred_element_type=jnp.float32)
    spare_high = spare_out.astype(jnp.bfloat16)
    spare_low = (spare_out - spare_high.astype(jnp.float32)).astype(jnp.bfloat16)

    home_at, home_scale = per_token(home_kept, home_flat, gate_weight, group_tokens, top_count)
    spare_at, spare_scale = per_token(spare_kept, spare_flat, gate_weight, group_tokens, top_count)
    home_pick = one_hot(home_at, slot_rows)
    spare_pick = one_hot(spare_at, slot_rows)
    home_term = jnp.dot(home_pick, home_out, preferred_element_type=jnp.float32)
    spare_term = jnp.dot(
        jnp.concatenate([spare_pick, spare_pick], axis=1),
        jnp.concatenate([spare_high, spare_low], axis=0),
        preferred_element_type=jnp.float32,
    )
    partial = home_scale[:, None] * home_term + spare_scale[:, None] * spare_term
    mixed = lax.psum_scatter(partial.astype(jnp.bfloat16), "ep", scatter_dimension=0, tiled=True)
    return mixed.astype(jnp.bfloat16)


def solution(mesh):
    return jax.shard_map(
        per_device,
        mesh=mesh,
        in_specs=(
            P("ep", "dp"),
            P("ep", None),
            P("ep", None),
            P(),
            P(),
            P("ep", None, None, "dp"),
            P("ep", None, "dp"),
            P("ep", None, None, "dp"),
            P("ep", None, "dp"),
        ),
        out_specs=P("ep", "dp"),
        check_vma=False,
    )
```

```python
import jax
import jax.numpy as jnp
from jax import lax
from jax.sharding import PartitionSpec as P


def gate_up(row_block, weight):
    gate_both = jnp.einsum("rd,djf->rjf", row_block, weight, preferred_element_type=jnp.float32)
    return (jax.nn.silu(gate_both[:, 0, :]) * gate_both[:, 1, :]).astype(jnp.bfloat16)


def slot_tables(ids, target, low, limit, capacity, top_count, gate_weight):
    groups, per_group = ids.shape
    group_tokens = per_group // top_count
    hit = ids == target
    ordinal = jnp.arange(per_group, dtype=jnp.int32)
    earlier = (ordinal[None, :] < ordinal[:, None]).astype(jnp.bfloat16)
    rank = jnp.einsum(
        "pq,gq->gp", earlier, hit.astype(jnp.bfloat16), preferred_element_type=jnp.float32
    ).astype(jnp.int32)
    position = rank - low
    kept = hit & (position >= 0) & (position < limit)
    slots = jnp.arange(capacity, dtype=jnp.int32)
    sel = kept[:, :, None] & (position[:, :, None] == slots[None, None, :])
    holds = jnp.any(sel.reshape(groups, group_tokens, top_count, capacity), axis=2)
    pick = jnp.transpose(holds, (0, 2, 1)).astype(jnp.bfloat16)
    scale = jnp.sum(
        jnp.where(kept.reshape(groups * group_tokens, top_count), gate_weight, 0.0), axis=1
    )
    return pick, holds.astype(jnp.bfloat16), scale


def side_columns(expert_ids, gate_logits):
    high = gate_logits.astype(jnp.bfloat16)
    rest = gate_logits - high.astype(jnp.float32)
    middle = rest.astype(jnp.bfloat16)
    low = (rest - middle.astype(jnp.float32)).astype(jnp.bfloat16)
    columns = jnp.concatenate([expert_ids.astype(jnp.bfloat16), high, middle, low], axis=1)
    width = -columns.shape[1] % 128
    return jnp.pad(columns, ((0, 0), (0, width)))


def gather_dp(block, axis):
    if lax.axis_size("dp") != 2:
        return lax.all_gather(block, "dp", axis=axis, tiled=True)
    partner = lax.ppermute(block, "dp", perm=[(0, 1), (1, 0)])
    first = lax.axis_index("dp") == 0
    low = jnp.where(first, block, partner)
    high = jnp.where(first, partner, block)
    return jnp.concatenate([low, high], axis=axis)


def per_device(
    tokens,
    expert_ids,
    gate_logits,
    placement,
    split_rows,
    gate_up_weight,
    down_weight,
    spare_gate_up,
    spare_down,
):
    ep_count = lax.axis_size("ep")
    me = lax.axis_index("ep")
    group_tokens = tokens.shape[0]
    top_count = expert_ids.shape[1]
    spares = placement.shape[0]
    halves = spare_gate_up.shape[0] * ep_count // spares
    capacity = group_tokens * top_count // ep_count
    per_group = group_tokens * top_count

    d_model = tokens.shape[1] * lax.axis_size("dp")
    whole_rows = gather_dp(tokens, 1)
    packed = jnp.concatenate([whole_rows, side_columns(expert_ids, gate_logits)], axis=1)
    every_row = lax.all_gather(packed, "ep", axis=0, tiled=True)
    all_tokens = every_row.shape[0]
    ids = every_row[:, d_model : d_model + top_count].astype(jnp.int32)
    parts = every_row[:, d_model + top_count : d_model + 4 * top_count].astype(jnp.float32)
    every_logit = (
        parts[:, :top_count] + parts[:, top_count : 2 * top_count]
    ) + parts[:, 2 * top_count :]
    ids = ids.reshape(ep_count, per_group)

    gate_score = jax.nn.sigmoid(every_logit)
    gate_weight = 2.5 * gate_score / jnp.sum(gate_score, axis=1, keepdims=True)

    is_match = placement == me
    home_limit = jnp.where(
        jnp.any(is_match), jnp.minimum(jnp.sum(jnp.where(is_match, split_rows, 0)), capacity), capacity
    )
    home_pick, home_take, home_scale = slot_tables(
        ids, me, 0, home_limit, capacity, top_count, gate_weight
    )
    spare_index = me // halves
    spare_pick, spare_take, spare_scale = slot_tables(
        ids,
        placement[spare_index],
        split_rows[spare_index],
        capacity,
        capacity,
        top_count,
        gate_weight,
    )

    grouped = every_row.reshape(ep_count, group_tokens, -1)
    slot_rows = ep_count * capacity
    home_rows = jnp.einsum(
        "gpi,gic->gpc", home_pick, grouped, preferred_element_type=jnp.float32
    ).astype(jnp.bfloat16).reshape(slot_rows, -1)
    spare_rows = jnp.einsum(
        "gpi,gic->gpc", spare_pick, grouped, preferred_element_type=jnp.float32
    ).astype(jnp.bfloat16).reshape(slot_rows, -1)
    home_hidden = gate_up(home_rows[:, :d_model], gate_up_weight[0])
    spare_hidden = gate_up(spare_rows[:, :d_model], spare_gate_up[0])
    home_hidden = lax.all_gather(home_hidden, "dp", axis=1, tiled=True)
    spare_hidden = gather_dp(spare_hidden, 1)
    home_out = jnp.dot(home_hidden, down_weight[0], preferred_element_type=jnp.float32)
    home_out = home_out.astype(jnp.bfloat16).reshape(ep_count, capacity, -1)
    spare_out = jnp.dot(spare_hidden, spare_down[0], preferred_element_type=jnp.float32)
    spare_high = spare_out.astype(jnp.bfloat16)
    spare_low = (spare_out - spare_high.astype(jnp.float32)).astype(jnp.bfloat16)
    spare_high = spare_high.reshape(ep_count, capacity, -1)
    spare_low = spare_low.reshape(ep_count, capacity, -1)

    home_term = jnp.einsum(
        "gip,gpc->gic", home_take, home_out, preferred_element_type=jnp.float32
    ).reshape(all_tokens, -1)
    spare_term = jnp.einsum(
        "gip,gpc->gic",
        jnp.concatenate([spare_take, spare_take], axis=2),
        jnp.concatenate([spare_high, spare_low], axis=1),
        preferred_element_type=jnp.float32,
    ).reshape(all_tokens, -1)
    partial = home_scale[:, None] * home_term + spare_scale[:, None] * spare_term
    mixed = lax.psum_scatter(partial.astype(jnp.bfloat16), "ep", scatter_dimension=0, tiled=True)
    return mixed.astype(jnp.bfloat16)


def solution(mesh):
    return jax.shard_map(
        per_device,
        mesh=mesh,
        in_specs=(
            P("ep", "dp"),
            P("ep", None),
            P("ep", None),
            P(),
            P(),
            P("ep", None, None, "dp"),
            P("ep", None, "dp"),
            P("ep", None, None, "dp"),
            P("ep", None, "dp"),
        ),
        out_specs=P("ep", "dp"),
        check_vma=False,
    )
```

```python
import jax
import jax.numpy as jnp
from jax import lax
from jax.sharding import PartitionSpec as P


def gate_up(row_block, weight):
    gate_both = jnp.einsum("rd,djf->rjf", row_block, weight, preferred_element_type=jnp.float32)
    return (jax.nn.silu(gate_both[:, 0, :]) * gate_both[:, 1, :]).astype(jnp.bfloat16)


def slot_tables(ids, target, low, limit, capacity, top_count, gate_weight):
    groups, per_group = ids.shape
    group_tokens = per_group // top_count
    hit = ids == target
    ordinal = jnp.arange(per_group, dtype=jnp.int32)
    earlier = (ordinal[None, :] < ordinal[:, None]).astype(jnp.bfloat16)
    rank = jnp.einsum(
        "pq,gq->gp", earlier, hit.astype(jnp.bfloat16), preferred_element_type=jnp.float32
    ).astype(jnp.int32)
    position = rank - low
    kept = hit & (position >= 0) & (position < limit)
    slots = jnp.arange(capacity, dtype=jnp.int32)
    sel = kept[:, :, None] & (position[:, :, None] == slots[None, None, :])
    holds = jnp.any(sel.reshape(groups, group_tokens, top_count, capacity), axis=2)
    pick = jnp.transpose(holds, (0, 2, 1)).astype(jnp.bfloat16)
    scale = jnp.sum(
        jnp.where(kept.reshape(groups * group_tokens, top_count), gate_weight, 0.0), axis=1
    )
    return pick, holds.astype(jnp.bfloat16), scale


def side_columns(expert_ids, gate_logits):
    high = gate_logits.astype(jnp.bfloat16)
    rest = gate_logits - high.astype(jnp.float32)
    middle = rest.astype(jnp.bfloat16)
    low = (rest - middle.astype(jnp.float32)).astype(jnp.bfloat16)
    columns = jnp.concatenate([expert_ids.astype(jnp.bfloat16), high, middle, low], axis=1)
    width = -columns.shape[1] % 128
    return jnp.pad(columns, ((0, 0), (0, width)))


def gather_dp(block, axis):
    if lax.axis_size("dp") != 2:
        return lax.all_gather(block, "dp", axis=axis, tiled=True)
    partner = lax.ppermute(block, "dp", perm=[(0, 1), (1, 0)])
    first = lax.axis_index("dp") == 0
    low = jnp.where(first, block, partner)
    high = jnp.where(first, partner, block)
    return jnp.concatenate([low, high], axis=axis)


def per_device(
    tokens,
    expert_ids,
    gate_logits,
    placement,
    split_rows,
    gate_up_weight,
    down_weight,
    spare_gate_up,
    spare_down,
):
    ep_count = lax.axis_size("ep")
    me = lax.axis_index("ep")
    group_tokens = tokens.shape[0]
    top_count = expert_ids.shape[1]
    spares = placement.shape[0]
    halves = spare_gate_up.shape[0] * ep_count // spares
    capacity = group_tokens * top_count // ep_count
    per_group = group_tokens * top_count

    d_model = tokens.shape[1] * lax.axis_size("dp")
    whole_rows = gather_dp(tokens, 1)
    packed = jnp.concatenate([whole_rows, side_columns(expert_ids, gate_logits)], axis=1)
    every_row = lax.all_gather(packed, "ep", axis=0, tiled=True)
    all_tokens = every_row.shape[0]
    ids = every_row[:, d_model : d_model + top_count].astype(jnp.int32)
    parts = every_row[:, d_model + top_count : d_model + 4 * top_count].astype(jnp.float32)
    every_logit = (
        parts[:, :top_count] + parts[:, top_count : 2 * top_count]
    ) + parts[:, 2 * top_count :]
    ids = ids.reshape(ep_count, per_group)

    gate_score = jax.nn.sigmoid(every_logit)
    gate_weight = 2.5 * gate_score / jnp.sum(gate_score, axis=1, keepdims=True)

    is_match = placement == me
    home_limit = jnp.where(
        jnp.any(is_match), jnp.minimum(jnp.sum(jnp.where(is_match, split_rows, 0)), capacity), capacity
    )
    home_pick, home_take, home_scale = slot_tables(
        ids, me, 0, home_limit, capacity, top_count, gate_weight
    )
    spare_index = me // halves
    spare_pick, spare_take, spare_scale = slot_tables(
        ids,
        placement[spare_index],
        split_rows[spare_index],
        capacity,
        capacity,
        top_count,
        gate_weight,
    )

    grouped = every_row.reshape(ep_count, group_tokens, -1)
    slot_rows = ep_count * capacity
    home_rows = jnp.einsum(
        "gpi,gic->gpc", home_pick, grouped, preferred_element_type=jnp.float32
    ).astype(jnp.bfloat16).reshape(slot_rows, -1)
    spare_rows = jnp.einsum(
        "gpi,gic->gpc", spare_pick, grouped, preferred_element_type=jnp.float32
    ).astype(jnp.bfloat16).reshape(slot_rows, -1)
    home_hidden = gate_up(home_rows[:, :d_model], gate_up_weight[0])
    spare_hidden = gate_up(spare_rows[:, :d_model], spare_gate_up[0])
    home_hidden = lax.all_gather(home_hidden, "dp", axis=1, tiled=True)
    spare_hidden = gather_dp(spare_hidden, 1)
    home_out = jnp.dot(home_hidden, down_weight[0], preferred_element_type=jnp.float32)
    home_out = home_out.astype(jnp.bfloat16).reshape(ep_count, capacity, -1)
    spare_out = jnp.dot(spare_hidden, spare_down[0], preferred_element_type=jnp.float32)
    spare_high = spare_out.astype(jnp.bfloat16)
    spare_low = (spare_out - spare_high.astype(jnp.float32)).astype(jnp.bfloat16)
    spare_high = spare_high.reshape(ep_count, capacity, -1)
    spare_low = spare_low.reshape(ep_count, capacity, -1)

    home_term = jnp.einsum(
        "gip,gpc->gic", home_take, home_out, preferred_element_type=jnp.float32
    ).reshape(all_tokens, -1)
    spare_term = jnp.einsum(
        "gip,gpc->gic",
        jnp.concatenate([spare_take, spare_take], axis=2),
        jnp.concatenate([spare_high, spare_low], axis=1),
        preferred_element_type=jnp.float32,
    ).reshape(all_tokens, -1)
    partial = home_scale[:, None] * home_term + spare_scale[:, None] * spare_term
    partial = partial.astype(jnp.bfloat16)
    split = partial.shape[1] // 2
    reduced = lax.psum_scatter(partial[:, :split], "ep", scatter_dimension=0, tiled=True)
    moved = lax.all_to_all(
        partial[:, split:].reshape(ep_count, group_tokens, -1), "ep", 0, 0, tiled=True
    )
    summed = jnp.sum(moved.astype(jnp.float32), axis=0)
    return jnp.concatenate([reduced, summed.astype(jnp.bfloat16)], axis=1)


def solution(mesh):
    return jax.shard_map(
        per_device,
        mesh=mesh,
        in_specs=(
            P("ep", "dp"),
            P("ep", None),
            P("ep", None),
            P(),
            P(),
            P("ep", None, None, "dp"),
            P("ep", None, "dp"),
            P("ep", None, None, "dp"),
            P("ep", None, "dp"),
        ),
        out_specs=P("ep", "dp"),
        check_vma=False,
    )
```

```python
import jax
import jax.numpy as jnp
from jax import lax
from jax.sharding import Mesh, PartitionSpec as P


def gate_up(row_block, weight):
    gate_both = jnp.einsum("rd,djf->rjf", row_block, weight, preferred_element_type=jnp.float32)
    return (jax.nn.silu(gate_both[:, 0, :]) * gate_both[:, 1, :]).astype(jnp.bfloat16)


def slot_tables(ids, target, low, limit, capacity, top_count, gate_weight):
    groups, per_group = ids.shape
    group_tokens = per_group // top_count
    hit = ids == target
    ordinal = jnp.arange(per_group, dtype=jnp.int32)
    earlier = (ordinal[None, :] < ordinal[:, None]).astype(jnp.bfloat16)
    rank = jnp.einsum(
        "pq,gq->gp", earlier, hit.astype(jnp.bfloat16), preferred_element_type=jnp.float32
    ).astype(jnp.int32)
    position = rank - low
    kept = hit & (position >= 0) & (position < limit)
    slots = jnp.arange(capacity, dtype=jnp.int32)
    sel = kept[:, :, None] & (position[:, :, None] == slots[None, None, :])
    holds = jnp.any(sel.reshape(groups, group_tokens, top_count, capacity), axis=2)
    pick = jnp.transpose(holds, (0, 2, 1)).astype(jnp.bfloat16)
    scale = jnp.sum(
        jnp.where(kept.reshape(groups * group_tokens, top_count), gate_weight, 0.0), axis=1
    )
    return pick, holds.astype(jnp.bfloat16), scale


def side_columns(expert_ids, gate_logits):
    high = gate_logits.astype(jnp.bfloat16)
    rest = gate_logits - high.astype(jnp.float32)
    middle = rest.astype(jnp.bfloat16)
    low = (rest - middle.astype(jnp.float32)).astype(jnp.bfloat16)
    columns = jnp.concatenate([expert_ids.astype(jnp.bfloat16), high, middle, low], axis=1)
    width = -columns.shape[1] % 128
    return jnp.pad(columns, ((0, 0), (0, width)))


def gather_dp(block, axis):
    if lax.axis_size("dp") != 2:
        return lax.all_gather(block, "dp", axis=axis, tiled=True)
    partner = lax.ppermute(block, "dp", perm=[(0, 1), (1, 0)])
    first = lax.axis_index("dp") == 0
    low = jnp.where(first, block, partner)
    high = jnp.where(first, partner, block)
    return jnp.concatenate([low, high], axis=axis)


def reduce_partial(partial, inner, group_tokens):
    if inner == 2:
        paired = partial.reshape(-1, 2, group_tokens, partial.shape[1])
        first = lax.axis_index("core") == 0
        keep = jnp.where(first, paired[:, 0], paired[:, 1])
        send = jnp.where(first, paired[:, 1], paired[:, 0])
        partial = (keep + lax.ppermute(send, "core", perm=[(0, 1), (1, 0)])).reshape(
            -1, partial.shape[1]
        )
        axes = "chip"
    else:
        axes = ("chip", "core")
    return lax.psum_scatter(
        partial.astype(jnp.bfloat16), axes, scatter_dimension=0, tiled=True
    ).astype(jnp.bfloat16)


def per_device(
    tokens,
    expert_ids,
    gate_logits,
    placement,
    split_rows,
    gate_up_weight,
    down_weight,
    spare_gate_up,
    spare_down,
):
    inner = lax.axis_size("core")
    ep_count = lax.axis_size("chip") * inner
    me = lax.axis_index("chip") * inner + lax.axis_index("core")
    group_tokens = tokens.shape[0]
    top_count = expert_ids.shape[1]
    spares = placement.shape[0]
    halves = spare_gate_up.shape[0] * ep_count // spares
    capacity = group_tokens * top_count // ep_count
    per_group = group_tokens * top_count

    d_model = tokens.shape[1] * lax.axis_size("dp")
    whole_rows = gather_dp(tokens, 1)
    packed = jnp.concatenate([whole_rows, side_columns(expert_ids, gate_logits)], axis=1)
    every_row = lax.all_gather(packed, ("chip", "core"), axis=0, tiled=True)
    all_tokens = every_row.shape[0]
    ids = every_row[:, d_model : d_model + top_count].astype(jnp.int32)
    parts = every_row[:, d_model + top_count : d_model + 4 * top_count].astype(jnp.float32)
    every_logit = (
        parts[:, :top_count] + parts[:, top_count : 2 * top_count]
    ) + parts[:, 2 * top_count :]
    ids = ids.reshape(ep_count, per_group)

    gate_score = jax.nn.sigmoid(every_logit)
    gate_weight = 2.5 * gate_score / jnp.sum(gate_score, axis=1, keepdims=True)

    is_match = placement == me
    home_limit = jnp.where(
        jnp.any(is_match), jnp.minimum(jnp.sum(jnp.where(is_match, split_rows, 0)), capacity), capacity
    )
    home_pick, home_take, home_scale = slot_tables(
        ids, me, 0, home_limit, capacity, top_count, gate_weight
    )
    spare_index = me // halves
    spare_pick, spare_take, spare_scale = slot_tables(
        ids,
        placement[spare_index],
        split_rows[spare_index],
        capacity,
        capacity,
        top_count,
        gate_weight,
    )

    grouped = every_row.reshape(ep_count, group_tokens, -1)
    slot_rows = ep_count * capacity
    home_rows = jnp.einsum(
        "gpi,gic->gpc", home_pick, grouped, preferred_element_type=jnp.float32
    ).astype(jnp.bfloat16).reshape(slot_rows, -1)
    spare_rows = jnp.einsum(
        "gpi,gic->gpc", spare_pick, grouped, preferred_element_type=jnp.float32
    ).astype(jnp.bfloat16).reshape(slot_rows, -1)
    home_hidden = gate_up(home_rows[:, :d_model], gate_up_weight[0])
    spare_hidden = gate_up(spare_rows[:, :d_model], spare_gate_up[0])
    home_hidden = lax.all_gather(home_hidden, "dp", axis=1, tiled=True)
    spare_hidden = gather_dp(spare_hidden, 1)
    home_out = jnp.dot(home_hidden, down_weight[0], preferred_element_type=jnp.float32)
    home_out = home_out.astype(jnp.bfloat16).reshape(ep_count, capacity, -1)
    spare_out = jnp.dot(spare_hidden, spare_down[0], preferred_element_type=jnp.float32)
    spare_high = spare_out.astype(jnp.bfloat16)
    spare_low = (spare_out - spare_high.astype(jnp.float32)).astype(jnp.bfloat16)
    spare_high = spare_high.reshape(ep_count, capacity, -1)
    spare_low = spare_low.reshape(ep_count, capacity, -1)

    home_term = jnp.einsum(
        "gip,gpc->gic", home_take, home_out, preferred_element_type=jnp.float32
    ).reshape(all_tokens, -1)
    spare_term = jnp.einsum(
        "gip,gpc->gic",
        jnp.concatenate([spare_take, spare_take], axis=2),
        jnp.concatenate([spare_high, spare_low], axis=1),
        preferred_element_type=jnp.float32,
    ).reshape(all_tokens, -1)
    partial = home_scale[:, None] * home_term + spare_scale[:, None] * spare_term
    return reduce_partial(partial, inner, group_tokens)


def solution(mesh):
    ep_count = mesh.shape["ep"]
    inner = 2 if ep_count % 2 == 0 else 1
    view = Mesh(
        mesh.devices.reshape(ep_count // inner, inner, mesh.shape["dp"]), ("chip", "core", "dp")
    )
    ep = ("chip", "core")
    return jax.shard_map(
        per_device,
        mesh=view,
        in_specs=(
            P(ep, "dp"),
            P(ep, None),
            P(ep, None),
            P(),
            P(),
            P(ep, None, None, "dp"),
            P(ep, None, "dp"),
            P(ep, None, None, "dp"),
            P(ep, None, "dp"),
        ),
        out_specs=P(ep, "dp"),
        check_vma=False,
    )
```

```python
import jax
import jax.numpy as jnp
from jax import lax
from jax.sharding import PartitionSpec as P


def gate_up(row_block, weight):
    gate_both = jnp.einsum("rd,djf->rjf", row_block, weight, preferred_element_type=jnp.float32)
    return (jax.nn.silu(gate_both[:, 0, :]) * gate_both[:, 1, :]).astype(jnp.bfloat16)


def slot_tables(ids, target, low, limit, capacity, top_count, gate_weight):
    groups, per_group = ids.shape
    group_tokens = per_group // top_count
    hit = ids == target
    ordinal = jnp.arange(per_group, dtype=jnp.int32)
    earlier = (ordinal[None, :] < ordinal[:, None]).astype(jnp.bfloat16)
    rank = jnp.einsum(
        "pq,gq->gp", earlier, hit.astype(jnp.bfloat16), preferred_element_type=jnp.float32
    ).astype(jnp.int32)
    position = rank - low
    kept = hit & (position >= 0) & (position < limit)
    slots = jnp.arange(capacity, dtype=jnp.int32)
    sel = kept[:, :, None] & (position[:, :, None] == slots[None, None, :])
    holds = jnp.any(sel.reshape(groups, group_tokens, top_count, capacity), axis=2)
    pick = jnp.transpose(holds, (0, 2, 1)).astype(jnp.bfloat16)
    scale = jnp.sum(
        jnp.where(kept.reshape(groups * group_tokens, top_count), gate_weight, 0.0), axis=1
    )
    return pick, holds.astype(jnp.bfloat16), scale


def side_columns(expert_ids, gate_logits):
    high = gate_logits.astype(jnp.bfloat16)
    rest = gate_logits - high.astype(jnp.float32)
    middle = rest.astype(jnp.bfloat16)
    low = (rest - middle.astype(jnp.float32)).astype(jnp.bfloat16)
    columns = jnp.concatenate([expert_ids.astype(jnp.bfloat16), high, middle, low], axis=1)
    width = -columns.shape[1] % 128
    return jnp.pad(columns, ((0, 0), (0, width)))


def gather_dp(block, axis):
    if lax.axis_size("dp") != 2:
        return lax.all_gather(block, "dp", axis=axis, tiled=True)
    partner = lax.ppermute(block, "dp", perm=[(0, 1), (1, 0)])
    first = lax.axis_index("dp") == 0
    low = jnp.where(first, block, partner)
    high = jnp.where(first, partner, block)
    return jnp.concatenate([low, high], axis=axis)


def per_device(
    tokens,
    expert_ids,
    gate_logits,
    placement,
    split_rows,
    gate_up_weight,
    down_weight,
    spare_gate_up,
    spare_down,
):
    ep_count = lax.axis_size("ep")
    me = lax.axis_index("ep")
    group_tokens = tokens.shape[0]
    top_count = expert_ids.shape[1]
    spares = placement.shape[0]
    halves = spare_gate_up.shape[0] * ep_count // spares
    capacity = group_tokens * top_count // ep_count
    per_group = group_tokens * top_count

    d_model = tokens.shape[1] * lax.axis_size("dp")
    whole_rows = gather_dp(tokens, 1)
    packed = jnp.concatenate([whole_rows, side_columns(expert_ids, gate_logits)], axis=1)
    every_row = lax.all_gather(packed, "ep", axis=0, tiled=True)
    all_tokens = every_row.shape[0]
    ids = every_row[:, d_model : d_model + top_count].astype(jnp.int32)
    parts = every_row[:, d_model + top_count : d_model + 4 * top_count].astype(jnp.float32)
    every_logit = (
        parts[:, :top_count] + parts[:, top_count : 2 * top_count]
    ) + parts[:, 2 * top_count :]
    ids = ids.reshape(ep_count, per_group)

    gate_score = jax.nn.sigmoid(every_logit)
    gate_weight = 2.5 * gate_score / jnp.sum(gate_score, axis=1, keepdims=True)

    is_match = placement == me
    home_limit = jnp.where(
        jnp.any(is_match), jnp.minimum(jnp.sum(jnp.where(is_match, split_rows, 0)), capacity), capacity
    )
    home_pick, home_take, home_scale = slot_tables(
        ids, me, 0, home_limit, capacity, top_count, gate_weight
    )
    spare_index = me // halves
    spare_pick, spare_take, spare_scale = slot_tables(
        ids,
        placement[spare_index],
        split_rows[spare_index],
        capacity,
        capacity,
        top_count,
        gate_weight,
    )

    grouped = every_row.reshape(ep_count, group_tokens, -1)
    slot_rows = ep_count * capacity
    home_rows = jnp.einsum(
        "gpi,gic->gpc", home_pick, grouped, preferred_element_type=jnp.float32
    ).astype(jnp.bfloat16).reshape(slot_rows, -1)
    spare_rows = jnp.einsum(
        "gpi,gic->gpc", spare_pick, grouped, preferred_element_type=jnp.float32
    ).astype(jnp.bfloat16).reshape(slot_rows, -1)
    home_hidden = gate_up(home_rows[:, :d_model], gate_up_weight[0])
    spare_hidden = gate_up(spare_rows[:, :d_model], spare_gate_up[0])
    home_hidden = gather_dp(home_hidden, 1)
    spare_hidden = gather_dp(spare_hidden, 1)
    home_out = jnp.dot(home_hidden, down_weight[0], preferred_element_type=jnp.float32)
    home_out = home_out.astype(jnp.bfloat16).reshape(ep_count, capacity, -1)
    spare_out = jnp.dot(spare_hidden, spare_down[0], preferred_element_type=jnp.float32)
    spare_high = spare_out.astype(jnp.bfloat16)
    spare_low = (spare_out - spare_high.astype(jnp.float32)).astype(jnp.bfloat16)
    spare_high = spare_high.reshape(ep_count, capacity, -1)
    spare_low = spare_low.reshape(ep_count, capacity, -1)

    home_term = jnp.einsum(
        "gip,gpc->gic", home_take, home_out, preferred_element_type=jnp.float32
    ).reshape(all_tokens, -1)
    spare_term = jnp.einsum(
        "gip,gpc->gic",
        jnp.concatenate([spare_take, spare_take], axis=2),
        jnp.concatenate([spare_high, spare_low], axis=1),
        preferred_element_type=jnp.float32,
    ).reshape(all_tokens, -1)
    partial = home_scale[:, None] * home_term + spare_scale[:, None] * spare_term
    mixed = lax.psum_scatter(partial.astype(jnp.bfloat16), "ep", scatter_dimension=0, tiled=True)
    return mixed.astype(jnp.bfloat16)


def solution(mesh):
    return jax.shard_map(
        per_device,
        mesh=mesh,
        in_specs=(
            P("ep", "dp"),
            P("ep", None),
            P("ep", None),
            P(),
            P(),
            P("ep", None, None, "dp"),
            P("ep", None, "dp"),
            P("ep", None, None, "dp"),
            P("ep", None, "dp"),
        ),
        out_specs=P("ep", "dp"),
        check_vma=False,
    )
```

```python
import jax
import jax.numpy as jnp
from jax import lax
from jax.sharding import PartitionSpec as P


def gate_up(row_block, weight):
    gate_both = jnp.einsum("rd,djf->rjf", row_block, weight, preferred_element_type=jnp.float32)
    return (jax.nn.silu(gate_both[:, 0, :]) * gate_both[:, 1, :]).astype(jnp.bfloat16)


def slot_tables(ids, target, low, limit, capacity, top_count, gate_weight):
    groups, per_group = ids.shape
    group_tokens = per_group // top_count
    hit = ids == target
    ordinal = jnp.arange(per_group, dtype=jnp.int32)
    earlier = (ordinal[None, :] < ordinal[:, None]).astype(jnp.bfloat16)
    rank = jnp.einsum(
        "pq,gq->gp", earlier, hit.astype(jnp.bfloat16), preferred_element_type=jnp.float32
    ).astype(jnp.int32)
    position = rank - low
    kept = hit & (position >= 0) & (position < limit)
    slots = jnp.arange(capacity, dtype=jnp.int32)
    sel = kept[:, :, None] & (position[:, :, None] == slots[None, None, :])
    holds = jnp.any(sel.reshape(groups, group_tokens, top_count, capacity), axis=2)
    pick = jnp.transpose(holds, (0, 2, 1)).astype(jnp.bfloat16)
    scale = jnp.sum(
        jnp.where(kept.reshape(groups * group_tokens, top_count), gate_weight, 0.0), axis=1
    )
    return pick, holds.astype(jnp.bfloat16), scale


def side_columns(expert_ids, gate_logits):
    high = gate_logits.astype(jnp.bfloat16)
    rest = gate_logits - high.astype(jnp.float32)
    middle = rest.astype(jnp.bfloat16)
    low = (rest - middle.astype(jnp.float32)).astype(jnp.bfloat16)
    columns = jnp.concatenate([expert_ids.astype(jnp.bfloat16), high, middle, low], axis=1)
    width = -columns.shape[1] % 128
    return jnp.pad(columns, ((0, 0), (0, width)))


def gather_dp(block, axis):
    if lax.axis_size("dp") != 2:
        return lax.all_gather(block, "dp", axis=axis, tiled=True)
    partner = lax.ppermute(block, "dp", perm=[(0, 1), (1, 0)])
    first = lax.axis_index("dp") == 0
    low = jnp.where(first, block, partner)
    high = jnp.where(first, partner, block)
    return jnp.concatenate([low, high], axis=axis)


def per_device(
    tokens,
    expert_ids,
    gate_logits,
    placement,
    split_rows,
    gate_up_weight,
    down_weight,
    spare_gate_up,
    spare_down,
):
    ep_count = lax.axis_size("ep")
    me = lax.axis_index("ep")
    group_tokens = tokens.shape[0]
    top_count = expert_ids.shape[1]
    spares = placement.shape[0]
    halves = spare_gate_up.shape[0] * ep_count // spares
    capacity = group_tokens * top_count // ep_count
    per_group = group_tokens * top_count

    d_model = tokens.shape[1] * lax.axis_size("dp")
    whole_rows = gather_dp(tokens, 1)
    packed = jnp.concatenate([whole_rows, side_columns(expert_ids, gate_logits)], axis=1)
    every_row = lax.all_gather(packed, "ep", axis=0, tiled=True)
    all_tokens = every_row.shape[0]
    ids = every_row[:, d_model : d_model + top_count].astype(jnp.int32)
    parts = every_row[:, d_model + top_count : d_model + 4 * top_count].astype(jnp.float32)
    every_logit = (
        parts[:, :top_count] + parts[:, top_count : 2 * top_count]
    ) + parts[:, 2 * top_count :]
    ids = ids.reshape(ep_count, per_group)

    gate_score = jax.nn.sigmoid(every_logit)
    gate_weight = 2.5 * gate_score / jnp.sum(gate_score, axis=1, keepdims=True)

    is_match = placement == me
    home_limit = jnp.where(
        jnp.any(is_match), jnp.minimum(jnp.sum(jnp.where(is_match, split_rows, 0)), capacity), capacity
    )
    home_pick, home_take, home_scale = slot_tables(
        ids, me, 0, home_limit, capacity, top_count, gate_weight
    )
    spare_index = me // halves
    spare_pick, spare_take, spare_scale = slot_tables(
        ids,
        placement[spare_index],
        split_rows[spare_index],
        capacity,
        capacity,
        top_count,
        gate_weight,
    )

    grouped = every_row.reshape(ep_count, group_tokens, -1)
    slot_rows = ep_count * capacity
    home_rows = jnp.einsum(
        "gpi,gic->gpc", home_pick, grouped, preferred_element_type=jnp.float32
    ).astype(jnp.bfloat16).reshape(slot_rows, -1)
    spare_rows = jnp.einsum(
        "gpi,gic->gpc", spare_pick, grouped, preferred_element_type=jnp.float32
    ).astype(jnp.bfloat16).reshape(slot_rows, -1)
    home_hidden = gate_up(home_rows[:, :d_model], gate_up_weight[0])
    home_hidden, spare_rows = lax.optimization_barrier((home_hidden, spare_rows))
    home_hidden = gather_dp(home_hidden, 1)
    spare_hidden = gather_dp(gate_up(spare_rows[:, :d_model], spare_gate_up[0]), 1)
    home_out = jnp.dot(home_hidden, down_weight[0], preferred_element_type=jnp.float32)
    home_out = home_out.astype(jnp.bfloat16).reshape(ep_count, capacity, -1)
    spare_out = jnp.dot(spare_hidden, spare_down[0], preferred_element_type=jnp.float32)
    spare_high = spare_out.astype(jnp.bfloat16)
    spare_low = (spare_out - spare_high.astype(jnp.float32)).astype(jnp.bfloat16)
    spare_high = spare_high.reshape(ep_count, capacity, -1)
    spare_low = spare_low.reshape(ep_count, capacity, -1)

    home_term = jnp.einsum(
        "gip,gpc->gic", home_take, home_out, preferred_element_type=jnp.float32
    ).reshape(all_tokens, -1)
    spare_term = jnp.einsum(
        "gip,gpc->gic",
        jnp.concatenate([spare_take, spare_take], axis=2),
        jnp.concatenate([spare_high, spare_low], axis=1),
        preferred_element_type=jnp.float32,
    ).reshape(all_tokens, -1)
    partial = home_scale[:, None] * home_term + spare_scale[:, None] * spare_term
    mixed = lax.psum_scatter(partial.astype(jnp.bfloat16), "ep", scatter_dimension=0, tiled=True)
    return mixed.astype(jnp.bfloat16)


def solution(mesh):
    return jax.shard_map(
        per_device,
        mesh=mesh,
        in_specs=(
            P("ep", "dp"),
            P("ep", None),
            P("ep", None),
            P(),
            P(),
            P("ep", None, None, "dp"),
            P("ep", None, "dp"),
            P("ep", None, None, "dp"),
            P("ep", None, "dp"),
        ),
        out_specs=P("ep", "dp"),
        check_vma=False,
    )
```

```python
import jax
import jax.numpy as jnp
from jax import lax
from jax.sharding import PartitionSpec as P


def gate_up(row_block, weight):
    gate_both = jnp.einsum("rd,djf->rjf", row_block, weight, preferred_element_type=jnp.float32)
    return (jax.nn.silu(gate_both[:, 0, :]) * gate_both[:, 1, :]).astype(jnp.bfloat16)


def slot_tables(ids, target, low, limit, capacity, top_count, gate_weight):
    groups, per_group = ids.shape
    group_tokens = per_group // top_count
    hit = ids == target
    ordinal = jnp.arange(per_group, dtype=jnp.int32)
    earlier = (ordinal[None, :] < ordinal[:, None]).astype(jnp.bfloat16)
    rank = jnp.einsum(
        "pq,gq->gp", earlier, hit.astype(jnp.bfloat16), preferred_element_type=jnp.float32
    ).astype(jnp.int32)
    position = rank - low
    kept = hit & (position >= 0) & (position < limit)
    slots = jnp.arange(capacity, dtype=jnp.int32)
    sel = kept[:, :, None] & (position[:, :, None] == slots[None, None, :])
    holds = jnp.any(sel.reshape(groups, group_tokens, top_count, capacity), axis=2)
    pick = jnp.transpose(holds, (0, 2, 1)).astype(jnp.bfloat16)
    scale = jnp.sum(
        jnp.where(kept.reshape(groups * group_tokens, top_count), gate_weight, 0.0), axis=1
    )
    return pick, holds.astype(jnp.bfloat16), scale


def side_columns(expert_ids, gate_logits):
    high = gate_logits.astype(jnp.bfloat16)
    rest = gate_logits - high.astype(jnp.float32)
    middle = rest.astype(jnp.bfloat16)
    low = (rest - middle.astype(jnp.float32)).astype(jnp.bfloat16)
    columns = jnp.concatenate([expert_ids.astype(jnp.bfloat16), high, middle, low], axis=1)
    width = -columns.shape[1] % 128
    return jnp.pad(columns, ((0, 0), (0, width)))


def gather_dp(block, axis):
    if lax.axis_size("dp") != 2:
        return lax.all_gather(block, "dp", axis=axis, tiled=True)
    partner = lax.ppermute(block, "dp", perm=[(0, 1), (1, 0)])
    first = lax.axis_index("dp") == 0
    low = jnp.where(first, block, partner)
    high = jnp.where(first, partner, block)
    return jnp.concatenate([low, high], axis=axis)


def per_device(
    tokens,
    expert_ids,
    gate_logits,
    placement,
    split_rows,
    gate_up_weight,
    down_weight,
    spare_gate_up,
    spare_down,
):
    ep_count = lax.axis_size("ep")
    me = lax.axis_index("ep")
    group_tokens = tokens.shape[0]
    top_count = expert_ids.shape[1]
    spares = placement.shape[0]
    halves = spare_gate_up.shape[0] * ep_count // spares
    capacity = group_tokens * top_count // ep_count
    per_group = group_tokens * top_count

    d_model = tokens.shape[1] * lax.axis_size("dp")
    whole_rows = gather_dp(tokens, 1)
    packed = jnp.concatenate([whole_rows, side_columns(expert_ids, gate_logits)], axis=1)
    every_row = lax.all_gather(packed, "ep", axis=0, tiled=True)
    all_tokens = every_row.shape[0]
    ids = every_row[:, d_model : d_model + top_count].astype(jnp.int32)
    parts = every_row[:, d_model + top_count : d_model + 4 * top_count].astype(jnp.float32)
    every_logit = (
        parts[:, :top_count] + parts[:, top_count : 2 * top_count]
    ) + parts[:, 2 * top_count :]
    ids = ids.reshape(ep_count, per_group)

    gate_score = jax.nn.sigmoid(every_logit)
    gate_weight = 2.5 * gate_score / jnp.sum(gate_score, axis=1, keepdims=True)

    is_match = placement == me
    home_limit = jnp.where(
        jnp.any(is_match), jnp.minimum(jnp.sum(jnp.where(is_match, split_rows, 0)), capacity), capacity
    )
    home_pick, home_take, home_scale = slot_tables(
        ids, me, 0, home_limit, capacity, top_count, gate_weight
    )
    spare_index = me // halves
    spare_pick, spare_take, spare_scale = slot_tables(
        ids,
        placement[spare_index],
        split_rows[spare_index],
        capacity,
        capacity,
        top_count,
        gate_weight,
    )

    grouped = every_row.reshape(ep_count, group_tokens, -1)
    slot_rows = ep_count * capacity
    rows = jnp.einsum(
        "gpi,gic->gpc",
        jnp.concatenate([home_pick, spare_pick], axis=1),
        grouped,
        preferred_element_type=jnp.float32,
    ).astype(jnp.bfloat16)
    home_rows = rows[:, :capacity].reshape(slot_rows, -1)
    spare_rows = rows[:, capacity:].reshape(slot_rows, -1)
    home_hidden = gate_up(home_rows[:, :d_model], gate_up_weight[0])
    home_hidden, spare_rows = lax.optimization_barrier((home_hidden, spare_rows))
    home_hidden = gather_dp(home_hidden, 1)
    spare_hidden = gather_dp(gate_up(spare_rows[:, :d_model], spare_gate_up[0]), 1)
    home_out = jnp.dot(home_hidden, down_weight[0], preferred_element_type=jnp.float32)
    home_out = home_out.astype(jnp.bfloat16).reshape(ep_count, capacity, -1)
    spare_out = jnp.dot(spare_hidden, spare_down[0], preferred_element_type=jnp.float32)
    spare_high = spare_out.astype(jnp.bfloat16)
    spare_low = (spare_out - spare_high.astype(jnp.float32)).astype(jnp.bfloat16)
    spare_high = spare_high.reshape(ep_count, capacity, -1)
    spare_low = spare_low.reshape(ep_count, capacity, -1)

    home_term = jnp.einsum(
        "gip,gpc->gic", home_take, home_out, preferred_element_type=jnp.float32
    ).reshape(all_tokens, -1)
    spare_term = jnp.einsum(
        "gip,gpc->gic",
        jnp.concatenate([spare_take, spare_take], axis=2),
        jnp.concatenate([spare_high, spare_low], axis=1),
        preferred_element_type=jnp.float32,
    ).reshape(all_tokens, -1)
    partial = home_scale[:, None] * home_term + spare_scale[:, None] * spare_term
    mixed = lax.psum_scatter(partial.astype(jnp.bfloat16), "ep", scatter_dimension=0, tiled=True)
    return mixed.astype(jnp.bfloat16)


def solution(mesh):
    return jax.shard_map(
        per_device,
        mesh=mesh,
        in_specs=(
            P("ep", "dp"),
            P("ep", None),
            P("ep", None),
            P(),
            P(),
            P("ep", None, None, "dp"),
            P("ep", None, "dp"),
            P("ep", None, None, "dp"),
            P("ep", None, "dp"),
        ),
        out_specs=P("ep", "dp"),
        check_vma=False,
    )
```

```python
import jax
import jax.numpy as jnp
from jax import lax
from jax.sharding import PartitionSpec as P


def gate_up(row_block, weight):
    units = weight.shape[2]
    gate_both = jnp.dot(
        row_block, weight.reshape(weight.shape[0], 2 * units), preferred_element_type=jnp.float32
    )
    return (jax.nn.silu(gate_both[:, :units]) * gate_both[:, units:]).astype(jnp.bfloat16)


def slot_tables(ids, target, low, limit, capacity, top_count, gate_weight):
    groups, per_group = ids.shape
    group_tokens = per_group // top_count
    hit = ids == target
    ordinal = jnp.arange(per_group, dtype=jnp.int32)
    earlier = (ordinal[None, :] < ordinal[:, None]).astype(jnp.bfloat16)
    rank = jnp.einsum(
        "pq,gq->gp", earlier, hit.astype(jnp.bfloat16), preferred_element_type=jnp.float32
    ).astype(jnp.int32)
    position = rank - low
    kept = hit & (position >= 0) & (position < limit)
    slots = jnp.arange(capacity, dtype=jnp.int32)
    sel = kept[:, :, None] & (position[:, :, None] == slots[None, None, :])
    holds = jnp.any(sel.reshape(groups, group_tokens, top_count, capacity), axis=2)
    pick = jnp.transpose(holds, (0, 2, 1)).astype(jnp.bfloat16)
    scale = jnp.sum(
        jnp.where(kept.reshape(groups * group_tokens, top_count), gate_weight, 0.0), axis=1
    )
    return pick, holds.astype(jnp.bfloat16), scale


def side_columns(expert_ids, gate_logits):
    high = gate_logits.astype(jnp.bfloat16)
    rest = gate_logits - high.astype(jnp.float32)
    middle = rest.astype(jnp.bfloat16)
    low = (rest - middle.astype(jnp.float32)).astype(jnp.bfloat16)
    columns = jnp.concatenate([expert_ids.astype(jnp.bfloat16), high, middle, low], axis=1)
    width = -columns.shape[1] % 128
    return jnp.pad(columns, ((0, 0), (0, width)))


def gather_dp(block, axis):
    if lax.axis_size("dp") != 2:
        return lax.all_gather(block, "dp", axis=axis, tiled=True)
    partner = lax.ppermute(block, "dp", perm=[(0, 1), (1, 0)])
    first = lax.axis_index("dp") == 0
    low = jnp.where(first, block, partner)
    high = jnp.where(first, partner, block)
    return jnp.concatenate([low, high], axis=axis)


def per_device(
    tokens,
    expert_ids,
    gate_logits,
    placement,
    split_rows,
    gate_up_weight,
    down_weight,
    spare_gate_up,
    spare_down,
):
    ep_count = lax.axis_size("ep")
    me = lax.axis_index("ep")
    group_tokens = tokens.shape[0]
    top_count = expert_ids.shape[1]
    spares = placement.shape[0]
    halves = spare_gate_up.shape[0] * ep_count // spares
    capacity = group_tokens * top_count // ep_count
    per_group = group_tokens * top_count

    d_model = tokens.shape[1] * lax.axis_size("dp")
    whole_rows = gather_dp(tokens, 1)
    packed = jnp.concatenate([whole_rows, side_columns(expert_ids, gate_logits)], axis=1)
    every_row = lax.all_gather(packed, "ep", axis=0, tiled=True)
    all_tokens = every_row.shape[0]
    ids = every_row[:, d_model : d_model + top_count].astype(jnp.int32)
    parts = every_row[:, d_model + top_count : d_model + 4 * top_count].astype(jnp.float32)
    every_logit = (
        parts[:, :top_count] + parts[:, top_count : 2 * top_count]
    ) + parts[:, 2 * top_count :]
    ids = ids.reshape(ep_count, per_group)

    gate_score = jax.nn.sigmoid(every_logit)
    gate_weight = 2.5 * gate_score / jnp.sum(gate_score, axis=1, keepdims=True)

    is_match = placement == me
    home_limit = jnp.where(
        jnp.any(is_match), jnp.minimum(jnp.sum(jnp.where(is_match, split_rows, 0)), capacity), capacity
    )
    home_pick, home_take, home_scale = slot_tables(
        ids, me, 0, home_limit, capacity, top_count, gate_weight
    )
    spare_index = me // halves
    spare_pick, spare_take, spare_scale = slot_tables(
        ids,
        placement[spare_index],
        split_rows[spare_index],
        capacity,
        capacity,
        top_count,
        gate_weight,
    )

    grouped = every_row.reshape(ep_count, group_tokens, -1)
    slot_rows = ep_count * capacity
    rows = jnp.einsum(
        "gpi,gic->gpc",
        jnp.concatenate([home_pick, spare_pick], axis=1),
        grouped,
        preferred_element_type=jnp.float32,
    ).astype(jnp.bfloat16)
    home_rows = rows[:, :capacity].reshape(slot_rows, -1)
    spare_rows = rows[:, capacity:].reshape(slot_rows, -1)
    home_hidden = gate_up(home_rows[:, :d_model], gate_up_weight[0])
    home_hidden, spare_rows = lax.optimization_barrier((home_hidden, spare_rows))
    home_hidden = gather_dp(home_hidden, 1)
    spare_hidden = gather_dp(gate_up(spare_rows[:, :d_model], spare_gate_up[0]), 1)
    home_out = jnp.dot(home_hidden, down_weight[0], preferred_element_type=jnp.float32)
    home_out = home_out.astype(jnp.bfloat16).reshape(ep_count, capacity, -1)
    spare_out = jnp.dot(spare_hidden, spare_down[0], preferred_element_type=jnp.float32)
    spare_high = spare_out.astype(jnp.bfloat16)
    spare_low = (spare_out - spare_high.astype(jnp.float32)).astype(jnp.bfloat16)
    spare_high = spare_high.reshape(ep_count, capacity, -1)
    spare_low = spare_low.reshape(ep_count, capacity, -1)

    home_term = jnp.einsum(
        "gip,gpc->gic", home_take, home_out, preferred_element_type=jnp.float32
    ).reshape(all_tokens, -1)
    spare_term = jnp.einsum(
        "gip,gpc->gic",
        jnp.concatenate([spare_take, spare_take], axis=2),
        jnp.concatenate([spare_high, spare_low], axis=1),
        preferred_element_type=jnp.float32,
    ).reshape(all_tokens, -1)
    partial = home_scale[:, None] * home_term + spare_scale[:, None] * spare_term
    mixed = lax.psum_scatter(partial.astype(jnp.bfloat16), "ep", scatter_dimension=0, tiled=True)
    return mixed.astype(jnp.bfloat16)


def solution(mesh):
    return jax.shard_map(
        per_device,
        mesh=mesh,
        in_specs=(
            P("ep", "dp"),
            P("ep", None),
            P("ep", None),
            P(),
            P(),
            P("ep", None, None, "dp"),
            P("ep", None, "dp"),
            P("ep", None, None, "dp"),
            P("ep", None, "dp"),
        ),
        out_specs=P("ep", "dp"),
        check_vma=False,
    )
```

```python
import jax
import jax.numpy as jnp
from jax import lax
from jax.sharding import PartitionSpec as P


def gate_up(row_block, weight):
    gate_both = jnp.einsum("rd,djf->rjf", row_block, weight, preferred_element_type=jnp.float32)
    return (jax.nn.silu(gate_both[:, 0, :]) * gate_both[:, 1, :]).astype(jnp.bfloat16)


def slot_tables(ids, target, low, limit, capacity, top_count, gate_weight):
    groups, per_group = ids.shape
    group_tokens = per_group // top_count
    hit = ids == target
    ordinal = jnp.arange(per_group, dtype=jnp.int32)
    earlier = (ordinal[None, :] < ordinal[:, None]).astype(jnp.bfloat16)
    rank = jnp.einsum(
        "pq,gq->gp", earlier, hit.astype(jnp.bfloat16), preferred_element_type=jnp.float32
    ).astype(jnp.int32)
    position = rank - low
    kept = hit & (position >= 0) & (position < limit)
    slots = jnp.arange(capacity, dtype=jnp.int32)
    sel = kept[:, :, None] & (position[:, :, None] == slots[None, None, :])
    holds = jnp.any(sel.reshape(groups, group_tokens, top_count, capacity), axis=2)
    pick = jnp.transpose(holds, (0, 2, 1)).astype(jnp.bfloat16)
    scale = jnp.sum(
        jnp.where(kept.reshape(groups * group_tokens, top_count), gate_weight, 0.0), axis=1
    )
    return pick, holds.astype(jnp.bfloat16), scale


def side_columns(expert_ids, gate_logits):
    high = gate_logits.astype(jnp.bfloat16)
    rest = gate_logits - high.astype(jnp.float32)
    middle = rest.astype(jnp.bfloat16)
    low = (rest - middle.astype(jnp.float32)).astype(jnp.bfloat16)
    columns = jnp.concatenate([expert_ids.astype(jnp.bfloat16), high, middle, low], axis=1)
    width = -columns.shape[1] % 128
    return jnp.pad(columns, ((0, 0), (0, width)))


def gather_dp(block, axis):
    if lax.axis_size("dp") != 2:
        return lax.all_gather(block, "dp", axis=axis, tiled=True)
    partner = lax.ppermute(block, "dp", perm=[(0, 1), (1, 0)])
    first = lax.axis_index("dp") == 0
    low = jnp.where(first, block, partner)
    high = jnp.where(first, partner, block)
    return jnp.concatenate([low, high], axis=axis)


def per_device(
    tokens,
    expert_ids,
    gate_logits,
    placement,
    split_rows,
    gate_up_weight,
    down_weight,
    spare_gate_up,
    spare_down,
):
    ep_count = lax.axis_size("ep")
    me = lax.axis_index("ep")
    group_tokens = tokens.shape[0]
    top_count = expert_ids.shape[1]
    spares = placement.shape[0]
    halves = spare_gate_up.shape[0] * ep_count // spares
    capacity = group_tokens * top_count // ep_count
    per_group = group_tokens * top_count

    d_model = tokens.shape[1] * lax.axis_size("dp")
    whole_rows = gather_dp(tokens, 1)
    packed = jnp.concatenate([whole_rows, side_columns(expert_ids, gate_logits)], axis=1)
    every_row = lax.all_gather(packed, "ep", axis=0, tiled=True)
    all_tokens = every_row.shape[0]
    ids = every_row[:, d_model : d_model + top_count].astype(jnp.int32)
    parts = every_row[:, d_model + top_count : d_model + 4 * top_count].astype(jnp.float32)
    every_logit = (
        parts[:, :top_count] + parts[:, top_count : 2 * top_count]
    ) + parts[:, 2 * top_count :]
    ids = ids.reshape(ep_count, per_group)

    gate_score = jax.nn.sigmoid(every_logit)
    gate_weight = 2.5 * gate_score / jnp.sum(gate_score, axis=1, keepdims=True)

    is_match = placement == me
    home_limit = jnp.where(
        jnp.any(is_match), jnp.minimum(jnp.sum(jnp.where(is_match, split_rows, 0)), capacity), capacity
    )
    home_pick, home_take, home_scale = slot_tables(
        ids, me, 0, home_limit, capacity, top_count, gate_weight
    )
    spare_index = me // halves
    spare_pick, spare_take, spare_scale = slot_tables(
        ids,
        placement[spare_index],
        split_rows[spare_index],
        capacity,
        capacity,
        top_count,
        gate_weight,
    )

    grouped = every_row.reshape(ep_count, group_tokens, -1)
    slot_rows = ep_count * capacity
    rows = jnp.einsum(
        "gpi,gic->gpc",
        jnp.concatenate([home_pick, spare_pick], axis=1),
        grouped,
        preferred_element_type=jnp.float32,
    ).astype(jnp.bfloat16)
    home_rows = rows[:, :capacity].reshape(slot_rows, -1)
    spare_rows = rows[:, capacity:].reshape(slot_rows, -1)
    half = slot_rows // 2
    first_hidden = gate_up(home_rows[:half, :d_model], gate_up_weight[0])
    first_hidden, home_rows = lax.optimization_barrier((first_hidden, home_rows))
    first_hidden = gather_dp(first_hidden, 1)
    second_hidden = gate_up(home_rows[half:, :d_model], gate_up_weight[0])
    second_hidden, spare_rows = lax.optimization_barrier((second_hidden, spare_rows))
    home_hidden = jnp.concatenate([first_hidden, gather_dp(second_hidden, 1)], axis=0)
    spare_hidden = gather_dp(gate_up(spare_rows[:, :d_model], spare_gate_up[0]), 1)
    home_out = jnp.dot(home_hidden, down_weight[0], preferred_element_type=jnp.float32)
    home_out = home_out.astype(jnp.bfloat16).reshape(ep_count, capacity, -1)
    spare_out = jnp.dot(spare_hidden, spare_down[0], preferred_element_type=jnp.float32)
    spare_high = spare_out.astype(jnp.bfloat16)
    spare_low = (spare_out - spare_high.astype(jnp.float32)).astype(jnp.bfloat16)
    spare_high = spare_high.reshape(ep_count, capacity, -1)
    spare_low = spare_low.reshape(ep_count, capacity, -1)

    home_term = jnp.einsum(
        "gip,gpc->gic", home_take, home_out, preferred_element_type=jnp.float32
    ).reshape(all_tokens, -1)
    spare_term = jnp.einsum(
        "gip,gpc->gic",
        jnp.concatenate([spare_take, spare_take], axis=2),
        jnp.concatenate([spare_high, spare_low], axis=1),
        preferred_element_type=jnp.float32,
    ).reshape(all_tokens, -1)
    partial = home_scale[:, None] * home_term + spare_scale[:, None] * spare_term
    mixed = lax.psum_scatter(partial.astype(jnp.bfloat16), "ep", scatter_dimension=0, tiled=True)
    return mixed.astype(jnp.bfloat16)


def solution(mesh):
    return jax.shard_map(
        per_device,
        mesh=mesh,
        in_specs=(
            P("ep", "dp"),
            P("ep", None),
            P("ep", None),
            P(),
            P(),
            P("ep", None, None, "dp"),
            P("ep", None, "dp"),
            P("ep", None, None, "dp"),
            P("ep", None, "dp"),
        ),
        out_specs=P("ep", "dp"),
        check_vma=False,
    )
```

```python
import jax
import jax.numpy as jnp
from jax import lax
from jax.sharding import PartitionSpec as P


def gate_up(row_block, weight):
    gate_both = jnp.einsum("rd,djf->rjf", row_block, weight, preferred_element_type=jnp.float32)
    return (jax.nn.silu(gate_both[:, 0, :]) * gate_both[:, 1, :]).astype(jnp.bfloat16)


def slot_tables(ids, target, low, limit, capacity, top_count, gate_weight):
    groups, per_group = ids.shape
    group_tokens = per_group // top_count
    hit = ids == target
    ordinal = jnp.arange(per_group, dtype=jnp.int32)
    earlier = (ordinal[None, :] < ordinal[:, None]).astype(jnp.bfloat16)
    rank = jnp.einsum(
        "pq,gq->gp", earlier, hit.astype(jnp.bfloat16), preferred_element_type=jnp.float32
    ).astype(jnp.int32)
    position = rank - low
    kept = hit & (position >= 0) & (position < limit)
    slots = jnp.arange(capacity, dtype=jnp.int32)
    sel = kept[:, :, None] & (position[:, :, None] == slots[None, None, :])
    holds = jnp.any(sel.reshape(groups, group_tokens, top_count, capacity), axis=2)
    pick = jnp.transpose(holds, (0, 2, 1)).astype(jnp.bfloat16)
    scale = jnp.sum(
        jnp.where(kept.reshape(groups * group_tokens, top_count), gate_weight, 0.0), axis=1
    )
    return pick, holds.astype(jnp.bfloat16), scale


def side_columns(expert_ids, gate_logits):
    high = gate_logits.astype(jnp.bfloat16)
    rest = gate_logits - high.astype(jnp.float32)
    middle = rest.astype(jnp.bfloat16)
    low = (rest - middle.astype(jnp.float32)).astype(jnp.bfloat16)
    columns = jnp.concatenate([expert_ids.astype(jnp.bfloat16), high, middle, low], axis=1)
    width = -columns.shape[1] % 128
    return jnp.pad(columns, ((0, 0), (0, width)))


def gather_dp(block, axis):
    if lax.axis_size("dp") != 2:
        return lax.all_gather(block, "dp", axis=axis, tiled=True)
    partner = lax.ppermute(block, "dp", perm=[(0, 1), (1, 0)])
    first = lax.axis_index("dp") == 0
    low = jnp.where(first, block, partner)
    high = jnp.where(first, partner, block)
    return jnp.concatenate([low, high], axis=axis)


def down_dp(hidden, weight):
    if lax.axis_size("dp") != 2:
        gathered = lax.all_gather(hidden, "dp", axis=1, tiled=True)
        return jnp.dot(gathered, weight, preferred_element_type=jnp.float32)
    partner = lax.ppermute(hidden, "dp", perm=[(0, 1), (1, 0)])
    blocks = weight.reshape(2, hidden.shape[1], weight.shape[1])
    first = lax.axis_index("dp") == 0
    own = jnp.where(first, blocks[0], blocks[1])
    other = jnp.where(first, blocks[1], blocks[0])
    return jnp.dot(hidden, own, preferred_element_type=jnp.float32) + jnp.dot(
        partner, other, preferred_element_type=jnp.float32
    )


def per_device(
    tokens,
    expert_ids,
    gate_logits,
    placement,
    split_rows,
    gate_up_weight,
    down_weight,
    spare_gate_up,
    spare_down,
):
    ep_count = lax.axis_size("ep")
    me = lax.axis_index("ep")
    group_tokens = tokens.shape[0]
    top_count = expert_ids.shape[1]
    spares = placement.shape[0]
    halves = spare_gate_up.shape[0] * ep_count // spares
    capacity = group_tokens * top_count // ep_count
    per_group = group_tokens * top_count

    d_model = tokens.shape[1] * lax.axis_size("dp")
    whole_rows = gather_dp(tokens, 1)
    packed = jnp.concatenate([whole_rows, side_columns(expert_ids, gate_logits)], axis=1)
    every_row = lax.all_gather(packed, "ep", axis=0, tiled=True)
    all_tokens = every_row.shape[0]
    ids = every_row[:, d_model : d_model + top_count].astype(jnp.int32)
    parts = every_row[:, d_model + top_count : d_model + 4 * top_count].astype(jnp.float32)
    every_logit = (
        parts[:, :top_count] + parts[:, top_count : 2 * top_count]
    ) + parts[:, 2 * top_count :]
    ids = ids.reshape(ep_count, per_group)

    gate_score = jax.nn.sigmoid(every_logit)
    gate_weight = 2.5 * gate_score / jnp.sum(gate_score, axis=1, keepdims=True)

    is_match = placement == me
    home_limit = jnp.where(
        jnp.any(is_match), jnp.minimum(jnp.sum(jnp.where(is_match, split_rows, 0)), capacity), capacity
    )
    home_pick, home_take, home_scale = slot_tables(
        ids, me, 0, home_limit, capacity, top_count, gate_weight
    )
    spare_index = me // halves
    spare_pick, spare_take, spare_scale = slot_tables(
        ids,
        placement[spare_index],
        split_rows[spare_index],
        capacity,
        capacity,
        top_count,
        gate_weight,
    )

    grouped = every_row.reshape(ep_count, group_tokens, -1)
    slot_rows = ep_count * capacity
    rows = jnp.einsum(
        "gpi,gic->gpc",
        jnp.concatenate([home_pick, spare_pick], axis=1),
        grouped,
        preferred_element_type=jnp.float32,
    ).astype(jnp.bfloat16)
    home_rows = rows[:, :capacity].reshape(slot_rows, -1)
    spare_rows = rows[:, capacity:].reshape(slot_rows, -1)
    home_hidden = gate_up(home_rows[:, :d_model], gate_up_weight[0])
    home_hidden, spare_rows = lax.optimization_barrier((home_hidden, spare_rows))
    home_out = down_dp(home_hidden, down_weight[0])
    home_out = home_out.astype(jnp.bfloat16).reshape(ep_count, capacity, -1)
    spare_out = down_dp(gate_up(spare_rows[:, :d_model], spare_gate_up[0]), spare_down[0])
    spare_high = spare_out.astype(jnp.bfloat16)
    spare_low = (spare_out - spare_high.astype(jnp.float32)).astype(jnp.bfloat16)
    spare_high = spare_high.reshape(ep_count, capacity, -1)
    spare_low = spare_low.reshape(ep_count, capacity, -1)

    home_term = jnp.einsum(
        "gip,gpc->gic", home_take, home_out, preferred_element_type=jnp.float32
    ).reshape(all_tokens, -1)
    spare_term = jnp.einsum(
        "gip,gpc->gic",
        jnp.concatenate([spare_take, spare_take], axis=2),
        jnp.concatenate([spare_high, spare_low], axis=1),
        preferred_element_type=jnp.float32,
    ).reshape(all_tokens, -1)
    partial = home_scale[:, None] * home_term + spare_scale[:, None] * spare_term
    mixed = lax.psum_scatter(partial.astype(jnp.bfloat16), "ep", scatter_dimension=0, tiled=True)
    return mixed.astype(jnp.bfloat16)


def solution(mesh):
    return jax.shard_map(
        per_device,
        mesh=mesh,
        in_specs=(
            P("ep", "dp"),
            P("ep", None),
            P("ep", None),
            P(),
            P(),
            P("ep", None, None, "dp"),
            P("ep", None, "dp"),
            P("ep", None, None, "dp"),
            P("ep", None, "dp"),
        ),
        out_specs=P("ep", "dp"),
        check_vma=False,
    )
```

```python
import jax
import jax.numpy as jnp
from jax import lax
from jax.sharding import PartitionSpec as P


def gate_up(row_block, weight):
    gate_both = jnp.einsum("rd,djf->rjf", row_block, weight, preferred_element_type=jnp.float32)
    return (jax.nn.silu(gate_both[:, 0, :]) * gate_both[:, 1, :]).astype(jnp.bfloat16)


def slot_tables(ids, target, low, limit, capacity, top_count, gate_weight):
    groups, per_group = ids.shape
    group_tokens = per_group // top_count
    hit = ids == target
    ordinal = jnp.arange(per_group, dtype=jnp.int32)
    earlier = (ordinal[None, :] < ordinal[:, None]).astype(jnp.bfloat16)
    rank = jnp.einsum(
        "pq,gq->gp", earlier, hit.astype(jnp.bfloat16), preferred_element_type=jnp.float32
    ).astype(jnp.int32)
    position = rank - low
    kept = hit & (position >= 0) & (position < limit)
    slots = jnp.arange(capacity, dtype=jnp.int32)
    sel = kept[:, :, None] & (position[:, :, None] == slots[None, None, :])
    holds = jnp.any(sel.reshape(groups, group_tokens, top_count, capacity), axis=2)
    pick = jnp.transpose(holds, (0, 2, 1)).astype(jnp.bfloat16)
    scale = jnp.sum(
        jnp.where(kept.reshape(groups * group_tokens, top_count), gate_weight, 0.0), axis=1
    )
    return pick, holds.astype(jnp.bfloat16), scale


def side_columns(expert_ids, gate_logits):
    high = gate_logits.astype(jnp.bfloat16)
    rest = gate_logits - high.astype(jnp.float32)
    middle = rest.astype(jnp.bfloat16)
    low = (rest - middle.astype(jnp.float32)).astype(jnp.bfloat16)
    columns = jnp.concatenate([expert_ids.astype(jnp.bfloat16), high, middle, low], axis=1)
    width = -columns.shape[1] % 128
    return jnp.pad(columns, ((0, 0), (0, width)))


def gather_dp(block, axis):
    if lax.axis_size("dp") != 2:
        return lax.all_gather(block, "dp", axis=axis, tiled=True)
    partner = lax.ppermute(block, "dp", perm=[(0, 1), (1, 0)])
    first = lax.axis_index("dp") == 0
    low = jnp.where(first, block, partner)
    high = jnp.where(first, partner, block)
    return jnp.concatenate([low, high], axis=axis)


def down_dp(hidden, weight):
    if lax.axis_size("dp") != 2:
        gathered = lax.all_gather(hidden, "dp", axis=1, tiled=True)
        return jnp.dot(gathered, weight, preferred_element_type=jnp.float32)
    partner = lax.ppermute(hidden, "dp", perm=[(0, 1), (1, 0)])
    blocks = weight.reshape(2, hidden.shape[1], weight.shape[1])
    first = lax.axis_index("dp") == 0
    own = jnp.where(first, blocks[0], blocks[1])
    other = jnp.where(first, blocks[1], blocks[0])
    return jnp.dot(hidden, own, preferred_element_type=jnp.float32) + jnp.dot(
        partner, other, preferred_element_type=jnp.float32
    )


def per_device(
    tokens,
    expert_ids,
    gate_logits,
    placement,
    split_rows,
    gate_up_weight,
    down_weight,
    spare_gate_up,
    spare_down,
):
    ep_count = lax.axis_size("ep")
    me = lax.axis_index("ep")
    group_tokens = tokens.shape[0]
    top_count = expert_ids.shape[1]
    spares = placement.shape[0]
    halves = spare_gate_up.shape[0] * ep_count // spares
    capacity = group_tokens * top_count // ep_count
    per_group = group_tokens * top_count

    d_model = tokens.shape[1] * lax.axis_size("dp")
    whole_rows = gather_dp(tokens, 1)
    packed = jnp.concatenate([whole_rows, side_columns(expert_ids, gate_logits)], axis=1)
    every_row = lax.all_gather(packed, "ep", axis=0, tiled=True)
    all_tokens = every_row.shape[0]
    ids = every_row[:, d_model : d_model + top_count].astype(jnp.int32)
    parts = every_row[:, d_model + top_count : d_model + 4 * top_count].astype(jnp.float32)
    every_logit = (
        parts[:, :top_count] + parts[:, top_count : 2 * top_count]
    ) + parts[:, 2 * top_count :]
    ids = ids.reshape(ep_count, per_group)

    gate_score = jax.nn.sigmoid(every_logit)
    gate_weight = 2.5 * gate_score / jnp.sum(gate_score, axis=1, keepdims=True)

    is_match = placement == me
    home_limit = jnp.where(
        jnp.any(is_match), jnp.minimum(jnp.sum(jnp.where(is_match, split_rows, 0)), capacity), capacity
    )
    home_pick, home_take, home_scale = slot_tables(
        ids, me, 0, home_limit, capacity, top_count, gate_weight
    )
    spare_index = me // halves
    spare_pick, spare_take, spare_scale = slot_tables(
        ids,
        placement[spare_index],
        split_rows[spare_index],
        capacity,
        capacity,
        top_count,
        gate_weight,
    )

    grouped = every_row.reshape(ep_count, group_tokens, -1)
    slot_rows = ep_count * capacity
    rows = jnp.einsum(
        "gpi,gic->gpc",
        jnp.concatenate([home_pick, spare_pick], axis=1),
        grouped,
        preferred_element_type=jnp.float32,
    ).astype(jnp.bfloat16)
    home_rows = rows[:, :capacity].reshape(slot_rows, -1)
    spare_rows = rows[:, capacity:].reshape(slot_rows, -1)
    home_hidden = gate_up(home_rows[:, :d_model], gate_up_weight[0])
    home_hidden, spare_rows = lax.optimization_barrier((home_hidden, spare_rows))
    home_out = down_dp(home_hidden, down_weight[0])
    home_out = home_out.astype(jnp.bfloat16).reshape(ep_count, capacity, -1)
    spare_out = down_dp(gate_up(spare_rows[:, :d_model], spare_gate_up[0]), spare_down[0])
    spare_high = spare_out.astype(jnp.bfloat16)
    spare_low = (spare_out - spare_high.astype(jnp.float32)).astype(jnp.bfloat16)
    spare_high = spare_high.reshape(ep_count, capacity, -1)
    spare_low = spare_low.reshape(ep_count, capacity, -1)

    home_term = jnp.einsum(
        "gip,gpc->gic", home_take, home_out, preferred_element_type=jnp.float32
    ).reshape(all_tokens, -1)
    spare_term = (
        jnp.einsum("gip,gpc->gic", spare_take, spare_high, preferred_element_type=jnp.float32)
        + jnp.einsum("gip,gpc->gic", spare_take, spare_low, preferred_element_type=jnp.float32)
    ).reshape(all_tokens, -1)
    partial = home_scale[:, None] * home_term + spare_scale[:, None] * spare_term
    mixed = lax.psum_scatter(partial.astype(jnp.bfloat16), "ep", scatter_dimension=0, tiled=True)
    return mixed.astype(jnp.bfloat16)


def solution(mesh):
    return jax.shard_map(
        per_device,
        mesh=mesh,
        in_specs=(
            P("ep", "dp"),
            P("ep", None),
            P("ep", None),
            P(),
            P(),
            P("ep", None, None, "dp"),
            P("ep", None, "dp"),
            P("ep", None, None, "dp"),
            P("ep", None, "dp"),
        ),
        out_specs=P("ep", "dp"),
        check_vma=False,
    )
```
